512 devices in a mesh: req: 128 (over z, y, core), wt: 4 (over x).
Axes of the slice: x: 4, y: 4, z: 16, core: 2. Of those that a mesh axis runs over, the one named last changes fastest.
Arguments:
- hidden_in: bfloat16 [32768, 5120], P('req', 'wt'), may hold values from -6 to 6
- queries: bfloat16 [32768, 5120], P('req', 'wt'), as said below
- key_proj: bfloat16 [32768, 5120], P('req', 'wt'), as said below
- values: bfloat16 [32768, 5120], P('req', 'wt'), may hold values from -6 to 6
- query_gain: float32 [5120], P('wt'), may hold values from 0.1 to 1.9
- key_gain: float32 [5120], P('wt'), may hold values from 0.1 to 1.9
- attn_gain: float32 [5120], P('wt'), may hold values from 0.1 to 1.9
- gate_w: bfloat16 [5120, 13824], P('wt', 'req'), may hold values from -0.078125 to 0.078125
- up_w: bfloat16 [5120, 13824], P('wt', 'req'), may hold values from -0.078125 to 0.078125
- lengths: int32 [128], replicated, may hold values from 1 to 256, 4608 in all
- assign: int32 [128], replicated, may hold values from 0 to 127, each once
- page_table: int32 [128, 2], P('req'), may hold values from 0 to 1, each once within a row
Outputs:
- gated: bfloat16 [128, 36, 13824], P(None, 'wt', 'req')
- key_cache: bfloat16 [256, 128, 5120], P('req', None, 'wt')
- value_cache: bfloat16 [256, 128, 5120], P('req', None, 'wt')
The draws below stay inside these ranges and needn't reach their ends.
Inputs may be any that keep to these rules, and one draw needn't show every extreme that they name: lengths sum to 4608 and at least one request has exactly 256 tokens. `assign`: each device of req serves exactly one request. `page_table`: each row names each of the 2 pages of one device once. `queries`: real-valued entries within -24 to 24. `key_proj`: real-valued entries within -24 to 24.
All inputs are finite; a program needn't handle non-finite values.
Results may differ from the reference program's by a relative error of at most 0.013.
Values may be sent and summed in bfloat16 or wider, within the bound.
No kernel may reach another device: no remote copies, remote signals or barrier semaphores. Data moves between devices by JAX's collectives and lax.ppermute only.
A program may use at most 128 MiB of HBM per device.

```python
import math
from functools import partial
import jax
import jax.numpy as jnp
import numpy as np
from jax import lax

D = 5120
HEADS = 40
HD = 128
FF = 13824
PAGE = 128
SLOTS = 256
LIVE = 36
OWNERS = 128
TOKENS = 32768
TOTAL = 4608
PAGES = 2


def column_scale():
    return 1.0 + 2.0 * jnp.arange(D, dtype=jnp.float32) / D


def draw_queries(key, part):
    base = jax.random.normal(jax.random.fold_in(key, 11), (TOKENS, D), jnp.float32) * column_scale()
    return jnp.clip(base, -24.0, 24.0).astype(jnp.bfloat16)


def draw_key_proj(key, part):
    base = jax.random.normal(jax.random.fold_in(key, 21), (TOKENS, D), jnp.float32) * column_scale()
    return jnp.clip(base, -24.0, 24.0).astype(jnp.bfloat16)


def shard_levels(stream_key, extent, split, low, high):
    gain = 1.0
    for dim, blocks in split:
        heights = jax.random.uniform(jax.random.fold_in(jax.random.fold_in(stream_key, 6), dim), (blocks,), jnp.float32, low / len(split), high / len(split))
        gain = gain * jnp.repeat(jnp.exp(heights), extent[dim] // blocks).reshape((-1,) + (1,) * (len(extent) - 1 - dim))
    return gain


def profile(count, total, limit, slope):
    weights = [(1 << 20) // math.isqrt(rank ** slope) + 1 for rank in range(2, count + 1)]
    surplus, holding = total - limit - (count - 1), [1] * (count - 1)
    while surplus > 0:
        candidates = [i for i in range(count - 1) if holding[i] < limit]
        mass, budget = sum([weights[i] for i in candidates]), surplus
        for i in candidates:
            more = min(limit - holding[i], max(1, budget * weights[i] // mass), surplus)
            holding[i] = holding[i] + more
            surplus = surplus - more
    return np.array([limit] + holding)


def uneven_parts(own_key, number_of, total, limit, skew):
    if number_of == 2:
        one = jax.random.randint(own_key, (), max(1, total - limit), min(limit, total - 1) + 1)
        return jnp.stack([one, total - one])
    sizes = jnp.asarray(profile(number_of, total, limit, skew), jnp.int32)
    twos = (number_of - 1) // 2
    giver, taker = sizes[1:1 + 2 * twos:2], sizes[2:2 + 2 * twos:2]
    slack = jnp.minimum(giver - 1, limit - taker)
    moved = jax.random.randint(jax.random.fold_in(own_key, 1), (twos,), 0, 1 << 20) % (slack + 1)
    sizes = sizes.at[1:1 + 2 * twos:2].set(giver - moved).at[2:2 + 2 * twos:2].set(taker + moved)
    return sizes[jax.random.permutation(jax.random.fold_in(own_key, 2), number_of)]


def centred(key, extent, scale, most, pieces=(), held_as=jnp.bfloat16):
    factor_of = shard_levels(key, extent, pieces, -0.22, 0.18) if pieces else 1.0
    drawn = jax.random.normal(key, extent, jnp.float32) * scale * factor_of
    return jnp.minimum(jnp.maximum(drawn, -most), most).astype(held_as)


def setup_inputs(seed: int = 0) -> dict:
    key_of = jax.random.split(jax.random.key(seed), 13)
    hidden_in = centred(key_of[0], (TOKENS, D), 1.0, 6.0, ((0, 128), (1, 4)))
    queries = draw_queries(jax.random.fold_in(key_of[12], 71), 0)
    key_proj = draw_key_proj(jax.random.fold_in(key_of[12], 71), 0)
    values = centred(key_of[3], (TOKENS, D), 1.0, 6.0, ((0, 128), (1, 4)))
    query_gain = jnp.clip(1.0 + 0.18 * jax.random.normal(key_of[4], (D,), jnp.float32), 0.1, 1.9)
    key_gain = jnp.clip(1.0 + 0.18 * jax.random.normal(key_of[5], (D,), jnp.float32), 0.1, 1.9)
    attn_gain = jnp.clip(1.0 + 0.18 * jax.random.normal(key_of[6], (D,), jnp.float32), 0.1, 1.9)
    gate_w = centred(key_of[7], (D, FF), D ** -0.5, 0.078125, ((0, 4), (1, 128)))
    up_w = centred(key_of[8], (D, FF), D ** -0.5, 0.078125, ((0, 4), (1, 128)))
    lengths = uneven_parts(key_of[9], OWNERS, TOTAL, SLOTS, 2).astype(jnp.int32)
    assign = jax.random.permutation(key_of[10], OWNERS).astype(jnp.int32)
    page_table = jax.vmap(lambda own: jax.random.permutation(own, PAGES))(jax.random.split(key_of[11], OWNERS)).reshape((OWNERS, PAGES)).astype(jnp.int32)
    return dict(hidden_in=hidden_in, queries=queries, key_proj=key_proj, values=values, query_gain=query_gain, key_gain=key_gain, attn_gain=attn_gain, gate_w=gate_w, up_w=up_w, lengths=lengths, assign=assign, page_table=page_table)


EPS = 1e-06
THETA = 500000.0

def rope_tables(row_count, head_width):
    half_width = head_width // 2
    frequency = THETA ** (-(jnp.arange(half_width, dtype=jnp.float32) * 2.0 / head_width))
    angles = jnp.arange(row_count, dtype=jnp.float32)[:, None] * frequency[None, :]
    return (jnp.cos(angles), jnp.sin(angles))

def rotate(heads_in, cosine, sine_table):
    half_width = heads_in.shape[-1] // 2
    leading = heads_in[..., :half_width]
    trailing = heads_in[..., half_width:]
    cos_b = cosine[:, None, :]
    sin_b = sine_table[:, None, :]
    return jnp.concatenate([leading * cos_b - trailing * sin_b, trailing * cos_b + leading * sin_b], axis=-1)

def rms_scale(field_in):
    return lax.rsqrt(lax.optimization_barrier(jnp.mean(field_in * field_in, axis=1, keepdims=True)) + EPS)

def owner_block(gains, block_in):
    query_gain, key_gain, attn_gain = gains
    hidden_rows, query_rows, key_rows, value_rows, length, placement = block_in
    query_f = query_rows.astype(jnp.float32)
    key_f = key_rows.astype(jnp.float32)
    query_n = query_f * rms_scale(query_f) * query_gain
    key_n = key_f * rms_scale(key_f) * key_gain
    cosine, sine_table = rope_tables(SLOTS, HD)
    query_r = rotate(query_n.reshape(SLOTS, HEADS, HD), cosine, sine_table).astype(jnp.bfloat16)
    key_r = rotate(key_n.reshape(SLOTS, HEADS, HD), cosine, sine_table).astype(jnp.bfloat16)
    scores = jnp.einsum('qhd,khd->hqk', query_r.astype(jnp.float32), key_r.astype(jnp.float32)) * HD ** (-0.5)
    position = jnp.arange(SLOTS, dtype=jnp.int32)
    allowed = (position[None, :] <= position[:, None]) & (position[None, :] < length)
    scores = jnp.where(allowed[None], scores, -jnp.inf)
    row_peak = lax.optimization_barrier(jnp.max(scores, axis=2, keepdims=True))
    expd = jnp.exp(scores - row_peak)
    probabilities = (expd / lax.optimization_barrier(jnp.sum(expd, axis=2, keepdims=True))).astype(jnp.bfloat16)
    value_heads = value_rows.reshape(SLOTS, HEADS, HD).astype(jnp.float32)
    attended = jnp.einsum('hqk,khd->qhd', probabilities.astype(jnp.float32), value_heads).astype(jnp.bfloat16).reshape(SLOTS, D)
    attended_f = attended.astype(jnp.float32)
    mixed_rows = (hidden_rows.astype(jnp.float32) + attended_f * rms_scale(attended_f) * attn_gain).astype(jnp.bfloat16)
    live_mask = (position < length)[:, None]
    zero_value = jnp.zeros((), jnp.bfloat16)
    key_pages = jnp.where(live_mask, key_r.reshape(SLOTS, D), zero_value).reshape(PAGES, PAGE, D)
    value_pages = jnp.where(live_mask, value_rows, zero_value).reshape(PAGES, PAGE, D)
    key_cache = jnp.zeros_like(key_pages).at[placement].set(key_pages)
    value_cache = jnp.zeros_like(value_pages).at[placement].set(value_pages)
    return (mixed_rows, key_cache, value_cache)

def reference(hidden_in, queries, key_proj, values, query_gain, key_gain, attn_gain, gate_w, up_w, lengths, assign, page_table):
    owner_req = jnp.zeros((OWNERS,), jnp.int32).at[assign].set(jnp.arange(OWNERS, dtype=jnp.int32))
    starts = (jnp.cumsum(lengths) - lengths).astype(jnp.int32)
    owner_len = lengths[owner_req].astype(jnp.int32)
    blocks = (hidden_in.reshape(OWNERS, SLOTS, D), queries.reshape(OWNERS, SLOTS, D), key_proj.reshape(OWNERS, SLOTS, D), values.reshape(OWNERS, SLOTS, D), owner_len, page_table)
    mixed_in, key_cache, value_cache = lax.map(partial(owner_block, (query_gain, key_gain, attn_gain)), blocks)
    arrival = jnp.arange(TOTAL, dtype=jnp.int32)
    request = (lax.optimization_barrier(jnp.sum((starts[None, :] <= arrival[:, None]).astype(jnp.int32), axis=1)) - 1).astype(jnp.int32)
    offset = (arrival - starts[request]).astype(jnp.int32)
    source_row = (assign[request] * SLOTS + offset).astype(jnp.int32)
    live_h = mixed_in.reshape(TOKENS, D)[source_row]
    gate_part = jnp.dot(live_h, gate_w, preferred_element_type=jnp.float32)
    up_part = jnp.dot(live_h, up_w, preferred_element_type=jnp.float32)
    gated = (jax.nn.silu(gate_part) * up_part).astype(jnp.bfloat16)
    gated = jnp.transpose(gated.reshape(LIVE, OWNERS, FF), (1, 0, 2))
    return (gated, key_cache.reshape(OWNERS * PAGES, PAGE, D), value_cache.reshape(OWNERS * PAGES, PAGE, D))
```

```python
import jax
import jax.numpy as jnp
from jax import lax
from jax.sharding import Mesh, PartitionSpec as P

D = 5120
HD = 128
PAGE = 128
LIVE = 36


EPS = 1e-06
THETA = 500000.0


def rope_tables(row_count, head_width):
    half_width = head_width // 2
    frequency = THETA ** (-(jnp.arange(half_width, dtype=jnp.float32) * 2.0 / head_width))
    angles = jnp.arange(row_count, dtype=jnp.float32)[:, None] * frequency[None, :]
    return (jnp.cos(angles), jnp.sin(angles))


def rotate(heads_in, cosine, sine_table):
    half_width = heads_in.shape[-1] // 2
    leading = heads_in[..., :half_width]
    trailing = heads_in[..., half_width:]
    cos_b = cosine[:, None, :]
    sin_b = sine_table[:, None, :]
    return jnp.concatenate(
        [leading * cos_b - trailing * sin_b, trailing * cos_b + leading * sin_b], axis=-1
    )


def deal_rows(source, owner_start, owner_len, device, owners, live_rows):
    slot_count = source.shape[0]
    feature_count = source.shape[1]
    per_peer = slot_count // owners
    column = jnp.arange(per_peer, dtype=jnp.int32)[None, :]
    target_dev = jnp.arange(owners, dtype=jnp.int32)[:, None]
    my_start = owner_start[device]
    my_length = owner_len[device]
    local_index = (target_dev - my_start) % owners + owners * column
    usable = local_index < my_length
    picked = jnp.where(
        usable[:, :, None],
        source[jnp.minimum(local_index, slot_count - 1)],
        jnp.zeros((), source.dtype),
    )
    arrived = lax.all_to_all(picked, ("ra", "rb"), split_axis=0, concat_axis=0, tiled=True)
    src_start = owner_start[:, None]
    src_length = owner_len[:, None]
    sent_index = (device - src_start) % owners + owners * column
    landing = jnp.where(
        sent_index < src_length, (src_start + sent_index - device) // owners, live_rows
    )
    packed = jnp.zeros((live_rows, feature_count), source.dtype)
    return packed.at[landing.reshape(-1)].set(arrived.reshape(-1, feature_count), mode="drop")


def per_device(
    hidden_in,
    queries,
    key_proj,
    values,
    query_gain,
    key_gain,
    attn_gain,
    gate_w,
    up_w,
    lengths,
    assign,
    page_table,
):
    slot_count = hidden_in.shape[0]
    feature_count = hidden_in.shape[1]
    owners = lax.axis_size(("ra", "rb"))
    device = lax.axis_index("ra") * lax.axis_size("rb") + lax.axis_index("rb")
    head_count = feature_count // HD
    unit_count = gate_w.shape[1]
    owner_req = jnp.zeros((owners,), jnp.int32).at[assign].set(jnp.arange(owners, dtype=jnp.int32))
    starts = jnp.cumsum(lengths) - lengths
    owner_start = starts[owner_req]
    owner_len = lengths[owner_req]
    my_length = owner_len[device]
    query_f = queries.astype(jnp.float32)
    key_f = key_proj.astype(jnp.float32)
    query_sq, key_sq = lax.psum(
        (jnp.sum(query_f * query_f, axis=1), jnp.sum(key_f * key_f, axis=1)), "wt"
    )
    query_n = query_f * lax.rsqrt(query_sq / D + EPS)[:, None] * query_gain
    key_n = key_f * lax.rsqrt(key_sq / D + EPS)[:, None] * key_gain
    cosine, sine_table = rope_tables(slot_count, HD)
    query_r = rotate(query_n.reshape(slot_count, head_count, HD), cosine, sine_table).astype(
        jnp.bfloat16
    )
    key_r = rotate(key_n.reshape(slot_count, head_count, HD), cosine, sine_table).astype(
        jnp.bfloat16
    )
    scores = jnp.einsum(
        "qhd,khd->hqk", query_r, key_r, preferred_element_type=jnp.float32
    ) * HD ** (-0.5)
    position = jnp.arange(slot_count, dtype=jnp.int32)
    allowed = (position[None, :] <= position[:, None]) & (position[None, :] < my_length)
    scores = jnp.where(allowed[None], scores, -jnp.inf)
    row_peak = jnp.max(scores, axis=2, keepdims=True)
    expd = jnp.exp(scores - row_peak)
    probabilities = (expd / jnp.sum(expd, axis=2, keepdims=True)).astype(jnp.bfloat16)
    value_heads = values.reshape(slot_count, head_count, HD)
    attended = jnp.einsum(
        "hqk,khd->qhd", probabilities, value_heads, preferred_element_type=jnp.float32
    )
    attended = attended.astype(jnp.bfloat16).reshape(slot_count, feature_count)
    attended_f = attended.astype(jnp.float32)
    attn_sq = lax.psum(jnp.sum(attended_f * attended_f, axis=1), "wt")
    layer_rows = (
        hidden_in.astype(jnp.float32)
        + attended_f * lax.rsqrt(attn_sq / D + EPS)[:, None] * attn_gain
    ).astype(jnp.bfloat16)
    live_mask = (position < my_length)[:, None]
    page_count = slot_count // PAGE
    zero_value = jnp.zeros((), jnp.bfloat16)
    key_pages = jnp.where(live_mask, key_r.reshape(slot_count, feature_count), zero_value).reshape(
        page_count, PAGE, feature_count
    )
    value_pages = jnp.where(live_mask, values, zero_value).reshape(page_count, PAGE, feature_count)
    placement = page_table[0]
    key_cache = jnp.zeros_like(key_pages).at[placement].set(key_pages)
    value_cache = jnp.zeros_like(value_pages).at[placement].set(value_pages)
    regrouped = deal_rows(layer_rows, owner_start, owner_len, device, owners, LIVE)
    outer = lax.axis_size("ra")
    inner = lax.axis_size("rb")
    piece = lax.all_gather(regrouped, "ra", axis=0, tiled=True)
    weights = lax.all_gather(jnp.stack([gate_w, up_w]), "rb", axis=2, tiled=True)
    stacked = jnp.einsum("tk,skn->tsn", piece, weights, preferred_element_type=jnp.float32)
    stacked = stacked.reshape(outer, LIVE, 2, inner * unit_count)
    summed = lax.psum_scatter(stacked, "wt", scatter_dimension=1, tiled=True)
    gated = (jax.nn.silu(summed[:, :, 0]) * summed[:, :, 1]).astype(jnp.bfloat16)
    rows_here = gated.shape[1]
    gated = gated.reshape(outer, rows_here, inner, unit_count)
    gated = lax.all_to_all(gated, "rb", split_axis=2, concat_axis=2, tiled=True)
    gated = jnp.transpose(gated, (0, 2, 1, 3)).reshape(outer * inner, rows_here, unit_count)
    return (gated, key_cache, value_cache)


def solution(mesh):
    inner = 4
    outer = mesh.shape["req"] // inner
    split = Mesh(mesh.devices.reshape(outer, inner, mesh.shape["wt"]), ("ra", "rb", "wt"))
    req = ("ra", "rb")
    placed = (
        P(req, "wt"),
        P(req, "wt"),
        P(req, "wt"),
        P(req, "wt"),
        P("wt"),
        P("wt"),
        P("wt"),
        P("wt", req),
        P("wt", req),
        P(),
        P(),
        P(req, None),
    )
    return jax.shard_map(
        per_device,
        mesh=split,
        in_specs=placed,
        out_specs=(P(None, "wt", req), P(req, None, "wt"), P(req, None, "wt")),
        check_vma=False,
    )
```

```python
import jax
import jax.numpy as jnp
from jax import lax
from jax.sharding import Mesh, PartitionSpec as P

D = 5120
HD = 128
PAGE = 128
LIVE = 36


EPS = 1e-06
THETA = 500000.0


def rope_tables(row_count, head_width):
    half_width = head_width // 2
    frequency = THETA ** (-(jnp.arange(half_width, dtype=jnp.float32) * 2.0 / head_width))
    angles = jnp.arange(row_count, dtype=jnp.float32)[:, None] * frequency[None, :]
    return (jnp.cos(angles), jnp.sin(angles))


def rotate(heads_in, cosine, sine_table):
    half_width = heads_in.shape[-1] // 2
    leading = heads_in[..., :half_width]
    trailing = heads_in[..., half_width:]
    cos_b = cosine[:, None, :]
    sin_b = sine_table[:, None, :]
    return jnp.concatenate(
        [leading * cos_b - trailing * sin_b, trailing * cos_b + leading * sin_b], axis=-1
    )


def deal_rows(source, owner_start, owner_len, device, owners, live_rows):
    slot_count = source.shape[0]
    feature_count = source.shape[1]
    per_peer = slot_count // owners
    column = jnp.arange(per_peer, dtype=jnp.int32)[None, :]
    target_dev = jnp.arange(owners, dtype=jnp.int32)[:, None]
    my_start = owner_start[device]
    my_length = owner_len[device]
    local_index = (target_dev - my_start) % owners + owners * column
    usable = local_index < my_length
    picked = jnp.where(
        usable[:, :, None],
        source[jnp.minimum(local_index, slot_count - 1)],
        jnp.zeros((), source.dtype),
    )
    arrived = lax.all_to_all(picked, ("ra", "rb"), split_axis=0, concat_axis=0, tiled=True)
    src_start = owner_start[:, None]
    src_length = owner_len[:, None]
    sent_index = (device - src_start) % owners + owners * column
    landing = jnp.where(
        sent_index < src_length, (src_start + sent_index - device) // owners, live_rows
    )
    packed = jnp.zeros((live_rows, feature_count), source.dtype)
    return packed.at[landing.reshape(-1)].set(arrived.reshape(-1, feature_count), mode="drop")


def per_device(
    hidden_in,
    queries,
    key_proj,
    values,
    query_gain,
    key_gain,
    attn_gain,
    gate_w,
    up_w,
    lengths,
    assign,
    page_table,
):
    slot_count = hidden_in.shape[0]
    feature_count = hidden_in.shape[1]
    owners = lax.axis_size(("ra", "rb"))
    device = lax.axis_index("ra") * lax.axis_size("rb") + lax.axis_index("rb")
    head_count = feature_count // HD
    unit_count = gate_w.shape[1]
    owner_req = jnp.zeros((owners,), jnp.int32).at[assign].set(jnp.arange(owners, dtype=jnp.int32))
    starts = jnp.cumsum(lengths) - lengths
    owner_start = starts[owner_req]
    owner_len = lengths[owner_req]
    my_length = owner_len[device]
    weights = lax.all_gather(jnp.stack([gate_w, up_w]), "ra", axis=2, tiled=True)
    query_f = queries.astype(jnp.float32)
    key_f = key_proj.astype(jnp.float32)
    query_sq, key_sq = lax.psum(
        (jnp.sum(query_f * query_f, axis=1), jnp.sum(key_f * key_f, axis=1)), "wt"
    )
    query_n = query_f * lax.rsqrt(query_sq / D + EPS)[:, None] * query_gain
    key_n = key_f * lax.rsqrt(key_sq / D + EPS)[:, None] * key_gain
    cosine, sine_table = rope_tables(slot_count, HD)
    query_r = rotate(query_n.reshape(slot_count, head_count, HD), cosine, sine_table).astype(
        jnp.bfloat16
    )
    key_r = rotate(key_n.reshape(slot_count, head_count, HD), cosine, sine_table).astype(
        jnp.bfloat16
    )
    scores = jnp.einsum(
        "qhd,khd->hqk", query_r, key_r, preferred_element_type=jnp.float32
    ) * HD ** (-0.5)
    position = jnp.arange(slot_count, dtype=jnp.int32)
    allowed = (position[None, :] <= position[:, None]) & (position[None, :] < my_length)
    scores = jnp.where(allowed[None], scores, -jnp.inf)
    row_peak = jnp.max(scores, axis=2, keepdims=True)
    expd = jnp.exp(scores - row_peak)
    probabilities = (expd / jnp.sum(expd, axis=2, keepdims=True)).astype(jnp.bfloat16)
    value_heads = values.reshape(slot_count, head_count, HD)
    attended = jnp.einsum(
        "hqk,khd->qhd", probabilities, value_heads, preferred_element_type=jnp.float32
    )
    attended = attended.astype(jnp.bfloat16).reshape(slot_count, feature_count)
    attended, weights = lax.optimization_barrier((attended, weights))
    attended_f = attended.astype(jnp.float32)
    attn_sq = lax.psum(jnp.sum(attended_f * attended_f, axis=1), "wt")
    layer_rows = (
        hidden_in.astype(jnp.float32)
        + attended_f * lax.rsqrt(attn_sq / D + EPS)[:, None] * attn_gain
    ).astype(jnp.bfloat16)
    live_mask = (position < my_length)[:, None]
    page_count = slot_count // PAGE
    zero_value = jnp.zeros((), jnp.bfloat16)
    key_pages = jnp.where(live_mask, key_r.reshape(slot_count, feature_count), zero_value).reshape(
        page_count, PAGE, feature_count
    )
    value_pages = jnp.where(live_mask, values, zero_value).reshape(page_count, PAGE, feature_count)
    placement = page_table[0]
    key_cache = jnp.zeros_like(key_pages).at[placement].set(key_pages)
    value_cache = jnp.zeros_like(value_pages).at[placement].set(value_pages)
    regrouped = deal_rows(layer_rows, owner_start, owner_len, device, owners, LIVE)
    outer = lax.axis_size("ra")
    inner = lax.axis_size("rb")
    piece = lax.all_gather(regrouped, "rb", axis=0, tiled=True)
    stacked = jnp.einsum("tk,skn->tsn", piece, weights, preferred_element_type=jnp.float32)
    stacked = stacked.reshape(inner, LIVE, 2, outer * unit_count)
    summed = lax.psum_scatter(stacked, "wt", scatter_dimension=1, tiled=True)
    gated = (jax.nn.silu(summed[:, :, 0]) * summed[:, :, 1]).astype(jnp.bfloat16)
    rows_here = gated.shape[1]
    gated = gated.reshape(inner, rows_here, outer, unit_count)
    gated = lax.all_to_all(gated, "ra", split_axis=2, concat_axis=2, tiled=True)
    gated = jnp.transpose(gated, (2, 0, 1, 3)).reshape(outer * inner, rows_here, unit_count)
    return (gated, key_cache, value_cache)


def solution(mesh):
    outer = 4
    inner = mesh.shape["req"] // outer
    split = Mesh(mesh.devices.reshape(outer, inner, mesh.shape["wt"]), ("ra", "rb", "wt"))
    req = ("ra", "rb")
    placed = (
        P(req, "wt"),
        P(req, "wt"),
        P(req, "wt"),
        P(req, "wt"),
        P("wt"),
        P("wt"),
        P("wt"),
        P("wt", req),
        P("wt", req),
        P(),
        P(),
        P(req, None),
    )
    return jax.shard_map(
        per_device,
        mesh=split,
        in_specs=placed,
        out_specs=(P(None, "wt", req), P(req, None, "wt"), P(req, None, "wt")),
        check_vma=False,
    )
```

```python
import jax
import jax.numpy as jnp
from jax import lax
from jax.sharding import Mesh, PartitionSpec as P

D = 5120
HD = 128
PAGE = 128
LIVE = 36


EPS = 1e-06
THETA = 500000.0


def rope_tables(row_count, head_width):
    half_width = head_width // 2
    frequency = THETA ** (-(jnp.arange(half_width, dtype=jnp.float32) * 2.0 / head_width))
    angles = jnp.arange(row_count, dtype=jnp.float32)[:, None] * frequency[None, :]
    return (jnp.cos(angles), jnp.sin(angles))


def rotate(heads_in, cosine, sine_table):
    half_width = heads_in.shape[-1] // 2
    leading = heads_in[..., :half_width]
    trailing = heads_in[..., half_width:]
    cos_b = cosine[:, None, :]
    sin_b = sine_table[:, None, :]
    return jnp.concatenate(
        [leading * cos_b - trailing * sin_b, trailing * cos_b + leading * sin_b], axis=-1
    )


def deal_rows(source, owner_start, owner_len, device, owners, live_rows):
    slot_count = source.shape[0]
    feature_count = source.shape[1]
    per_peer = slot_count // owners
    column = jnp.arange(per_peer, dtype=jnp.int32)[None, :]
    target_dev = jnp.arange(owners, dtype=jnp.int32)[:, None]
    my_start = owner_start[device]
    my_length = owner_len[device]
    local_index = (target_dev - my_start) % owners + owners * column
    usable = local_index < my_length
    picked = jnp.where(
        usable[:, :, None],
        source[jnp.minimum(local_index, slot_count - 1)],
        jnp.zeros((), source.dtype),
    )
    arrived = lax.all_to_all(picked, ("ra", "rb"), split_axis=0, concat_axis=0, tiled=True)
    src_start = owner_start[:, None]
    src_length = owner_len[:, None]
    sent_index = (device - src_start) % owners + owners * column
    landing = jnp.where(
        sent_index < src_length, (src_start + sent_index - device) // owners, live_rows
    )
    packed = jnp.zeros((live_rows, feature_count), source.dtype)
    return packed.at[landing.reshape(-1)].set(arrived.reshape(-1, feature_count), mode="drop")


def per_device(
    hidden_in,
    queries,
    key_proj,
    values,
    query_gain,
    key_gain,
    attn_gain,
    gate_w,
    up_w,
    lengths,
    assign,
    page_table,
):
    slot_count = hidden_in.shape[0]
    feature_count = hidden_in.shape[1]
    owners = lax.axis_size(("ra", "rb"))
    device = lax.axis_index("ra") * lax.axis_size("rb") + lax.axis_index("rb")
    head_count = feature_count // HD
    unit_count = gate_w.shape[1]
    owner_req = jnp.zeros((owners,), jnp.int32).at[assign].set(jnp.arange(owners, dtype=jnp.int32))
    starts = jnp.cumsum(lengths) - lengths
    owner_start = starts[owner_req]
    owner_len = lengths[owner_req]
    my_length = owner_len[device]
    weights = lax.all_gather(jnp.stack([gate_w, up_w]), "ra", axis=2, tiled=True)
    query_f = queries.astype(jnp.float32)
    key_f = key_proj.astype(jnp.float32)
    query_sq, key_sq = lax.psum(
        (jnp.sum(query_f * query_f, axis=1), jnp.sum(key_f * key_f, axis=1)), "wt"
    )
    query_n = query_f * lax.rsqrt(query_sq / D + EPS)[:, None] * query_gain
    key_n = key_f * lax.rsqrt(key_sq / D + EPS)[:, None] * key_gain
    cosine, sine_table = rope_tables(slot_count, HD)
    query_r = rotate(query_n.reshape(slot_count, head_count, HD), cosine, sine_table).astype(
        jnp.bfloat16
    )
    key_r = rotate(key_n.reshape(slot_count, head_count, HD), cosine, sine_table).astype(
        jnp.bfloat16
    )
    scores = jnp.einsum(
        "qhd,khd->hqk", query_r, key_r, preferred_element_type=jnp.float32
    ) * HD ** (-0.5)
    position = jnp.arange(slot_count, dtype=jnp.int32)
    allowed = (position[None, :] <= position[:, None]) & (position[None, :] < my_length)
    scores = jnp.where(allowed[None], scores, -jnp.inf)
    row_peak = jnp.max(scores, axis=2, keepdims=True)
    expd = jnp.exp(scores - row_peak)
    probabilities = (expd / jnp.sum(expd, axis=2, keepdims=True)).astype(jnp.bfloat16)
    value_heads = values.reshape(slot_count, head_count, HD)
    attended = jnp.einsum(
        "hqk,khd->qhd", probabilities, value_heads, preferred_element_type=jnp.float32
    )
    attended = attended.astype(jnp.bfloat16).reshape(slot_count, feature_count)
    attended_f = attended.astype(jnp.float32)
    attn_sq = lax.psum(jnp.sum(attended_f * attended_f, axis=1), "wt")
    layer_rows = (
        hidden_in.astype(jnp.float32)
        + attended_f * lax.rsqrt(attn_sq / D + EPS)[:, None] * attn_gain
    ).astype(jnp.bfloat16)
    live_mask = (position < my_length)[:, None]
    page_count = slot_count // PAGE
    zero_value = jnp.zeros((), jnp.bfloat16)
    key_pages = jnp.where(live_mask, key_r.reshape(slot_count, feature_count), zero_value).reshape(
        page_count, PAGE, feature_count
    )
    value_pages = jnp.where(live_mask, values, zero_value).reshape(page_count, PAGE, feature_count)
    placement = page_table[0]
    key_cache = jnp.zeros_like(key_pages).at[placement].set(key_pages)
    value_cache = jnp.zeros_like(value_pages).at[placement].set(value_pages)
    regrouped = deal_rows(layer_rows, owner_start, owner_len, device, owners, LIVE)
    regrouped, weights = lax.optimization_barrier((regrouped, weights))
    outer = lax.axis_size("ra")
    inner = lax.axis_size("rb")
    piece = lax.all_gather(regrouped, "rb", axis=0, tiled=True)
    stacked = jnp.einsum("tk,skn->tsn", piece, weights, preferred_element_type=jnp.float32)
    parts = lax.axis_size("wt")
    stacked = stacked.astype(jnp.bfloat16).reshape(inner, parts, LIVE // parts, 2, outer * unit_count)
    stacked = lax.all_to_all(stacked, "wt", split_axis=1, concat_axis=1, tiled=True)
    summed = jnp.sum(stacked.astype(jnp.float32), axis=1)
    gated = (jax.nn.silu(summed[:, :, 0]) * summed[:, :, 1]).astype(jnp.bfloat16)
    rows_here = gated.shape[1]
    gated = gated.reshape(inner, rows_here, outer, unit_count)
    gated = lax.all_to_all(gated, "ra", split_axis=2, concat_axis=2, tiled=True)
    gated = jnp.transpose(gated, (2, 0, 1, 3)).reshape(outer * inner, rows_here, unit_count)
    return (gated, key_cache, value_cache)


def solution(mesh):
    outer = 4
    inner = mesh.shape["req"] // outer
    split = Mesh(mesh.devices.reshape(outer, inner, mesh.shape["wt"]), ("ra", "rb", "wt"))
    req = ("ra", "rb")
    placed = (
        P(req, "wt"),
        P(req, "wt"),
        P(req, "wt"),
        P(req, "wt"),
        P("wt"),
        P("wt"),
        P("wt"),
        P("wt", req),
        P("wt", req),
        P(),
        P(),
        P(req, None),
    )
    return jax.shard_map(
        per_device,
        mesh=split,
        in_specs=placed,
        out_specs=(P(None, "wt", req), P(req, None, "wt"), P(req, None, "wt")),
        check_vma=False,
    )
```

```python
import jax
import jax.numpy as jnp
from jax import lax
from jax.sharding import Mesh, PartitionSpec as P

D = 5120
HD = 128
PAGE = 128
LIVE = 36


EPS = 1e-06
THETA = 500000.0


def rope_tables(row_count, head_width):
    half_width = head_width // 2
    frequency = THETA ** (-(jnp.arange(half_width, dtype=jnp.float32) * 2.0 / head_width))
    angles = jnp.arange(row_count, dtype=jnp.float32)[:, None] * frequency[None, :]
    return (jnp.cos(angles), jnp.sin(angles))


def rotate(heads_in, cosine, sine_table):
    half_width = heads_in.shape[-1] // 2
    leading = heads_in[..., :half_width]
    trailing = heads_in[..., half_width:]
    cos_b = cosine[:, None, :]
    sin_b = sine_table[:, None, :]
    return jnp.concatenate(
        [leading * cos_b - trailing * sin_b, trailing * cos_b + leading * sin_b], axis=-1
    )


def deal_rows(source, owner_start, owner_len, device, owners, live_rows):
    slot_count = source.shape[0]
    feature_count = source.shape[1]
    per_peer = slot_count // owners
    column = jnp.arange(per_peer, dtype=jnp.int32)[None, :]
    target_dev = jnp.arange(owners, dtype=jnp.int32)[:, None]
    my_start = owner_start[device]
    my_length = owner_len[device]
    local_index = (target_dev - my_start) % owners + owners * column
    usable = local_index < my_length
    picked = jnp.where(
        usable[:, :, None],
        source[jnp.minimum(local_index, slot_count - 1)],
        jnp.zeros((), source.dtype),
    )
    arrived = lax.all_to_all(picked, ("ra", "rb"), split_axis=0, concat_axis=0, tiled=True)
    src_start = owner_start[:, None]
    src_length = owner_len[:, None]
    sent_index = (device - src_start) % owners + owners * column
    landing = jnp.where(
        sent_index < src_length, (src_start + sent_index - device) // owners, live_rows
    )
    packed = jnp.zeros((live_rows, feature_count), source.dtype)
    return packed.at[landing.reshape(-1)].set(arrived.reshape(-1, feature_count), mode="drop")


def per_device(
    hidden_in,
    queries,
    key_proj,
    values,
    query_gain,
    key_gain,
    attn_gain,
    gate_w,
    up_w,
    lengths,
    assign,
    page_table,
):
    slot_count = hidden_in.shape[0]
    feature_count = hidden_in.shape[1]
    owners = lax.axis_size(("ra", "rb"))
    device = lax.axis_index("ra") * lax.axis_size("rb") + lax.axis_index("rb")
    head_count = feature_count // HD
    unit_count = gate_w.shape[1]
    owner_req = jnp.zeros((owners,), jnp.int32).at[assign].set(jnp.arange(owners, dtype=jnp.int32))
    starts = jnp.cumsum(lengths) - lengths
    owner_start = starts[owner_req]
    owner_len = lengths[owner_req]
    my_length = owner_len[device]
    weights = lax.all_gather(jnp.stack([gate_w, up_w]), "rb", axis=2, tiled=True)
    query_f = queries.astype(jnp.float32)
    key_f = key_proj.astype(jnp.float32)
    query_sq, key_sq = lax.psum(
        (jnp.sum(query_f * query_f, axis=1), jnp.sum(key_f * key_f, axis=1)), "wt"
    )
    query_n = query_f * lax.rsqrt(query_sq / D + EPS)[:, None] * query_gain
    key_n = key_f * lax.rsqrt(key_sq / D + EPS)[:, None] * key_gain
    cosine, sine_table = rope_tables(slot_count, HD)
    query_r = rotate(query_n.reshape(slot_count, head_count, HD), cosine, sine_table).astype(
        jnp.bfloat16
    )
    key_r = rotate(key_n.reshape(slot_count, head_count, HD), cosine, sine_table).astype(
        jnp.bfloat16
    )
    scores = jnp.einsum(
        "qhd,khd->hqk", query_r, key_r, preferred_element_type=jnp.float32
    ) * HD ** (-0.5)
    position = jnp.arange(slot_count, dtype=jnp.int32)
    allowed = (position[None, :] <= position[:, None]) & (position[None, :] < my_length)
    scores = jnp.where(allowed[None], scores, -jnp.inf)
    row_peak = jnp.max(scores, axis=2, keepdims=True)
    expd = jnp.exp(scores - row_peak)
    probabilities = (expd / jnp.sum(expd, axis=2, keepdims=True)).astype(jnp.bfloat16)
    value_heads = values.reshape(slot_count, head_count, HD)
    attended = jnp.einsum(
        "hqk,khd->qhd", probabilities, value_heads, preferred_element_type=jnp.float32
    )
    attended = attended.astype(jnp.bfloat16).reshape(slot_count, feature_count)
    attended_f = attended.astype(jnp.float32)
    attn_sq = lax.psum(jnp.sum(attended_f * attended_f, axis=1), "wt")
    layer_rows = (
        hidden_in.astype(jnp.float32)
        + attended_f * lax.rsqrt(attn_sq / D + EPS)[:, None] * attn_gain
    ).astype(jnp.bfloat16)
    live_mask = (position < my_length)[:, None]
    page_count = slot_count // PAGE
    zero_value = jnp.zeros((), jnp.bfloat16)
    key_pages = jnp.where(live_mask, key_r.reshape(slot_count, feature_count), zero_value).reshape(
        page_count, PAGE, feature_count
    )
    value_pages = jnp.where(live_mask, values, zero_value).reshape(page_count, PAGE, feature_count)
    placement = page_table[0]
    key_cache = jnp.zeros_like(key_pages).at[placement].set(key_pages)
    value_cache = jnp.zeros_like(value_pages).at[placement].set(value_pages)
    regrouped = deal_rows(layer_rows, owner_start, owner_len, device, owners, LIVE)
    regrouped, weights = lax.optimization_barrier((regrouped, weights))
    outer = lax.axis_size("ra")
    inner = lax.axis_size("rb")
    piece = lax.all_gather(regrouped, "ra", axis=0, tiled=True)
    stacked = jnp.einsum("tk,skn->tsn", piece, weights, preferred_element_type=jnp.float32)
    parts = lax.axis_size("wt")
    stacked = stacked.astype(jnp.bfloat16).reshape(outer, parts, LIVE // parts, 2, inner * unit_count)
    stacked = lax.all_to_all(stacked, "wt", split_axis=1, concat_axis=1, tiled=True)
    summed = jnp.sum(stacked.astype(jnp.float32), axis=1)
    gated = (jax.nn.silu(summed[:, :, 0]) * summed[:, :, 1]).astype(jnp.bfloat16)
    rows_here = gated.shape[1]
    gated = gated.reshape(outer, rows_here, inner, unit_count)
    gated = lax.all_to_all(gated, "rb", split_axis=2, concat_axis=2, tiled=True)
    gated = jnp.transpose(gated, (0, 2, 1, 3)).reshape(outer * inner, rows_here, unit_count)
    return (gated, key_cache, value_cache)


def solution(mesh):
    inner = 8
    outer = mesh.shape["req"] // inner
    split = Mesh(mesh.devices.reshape(outer, inner, mesh.shape["wt"]), ("ra", "rb", "wt"))
    req = ("ra", "rb")
    placed = (
        P(req, "wt"),
        P(req, "wt"),
        P(req, "wt"),
        P(req, "wt"),
        P("wt"),
        P("wt"),
        P("wt"),
        P("wt", req),
        P("wt", req),
        P(),
        P(),
        P(req, None),
    )
    return jax.shard_map(
        per_device,
        mesh=split,
        in_specs=placed,
        out_specs=(P(None, "wt", req), P(req, None, "wt"), P(req, None, "wt")),
        check_vma=False,
    )
```

```python
import jax
import jax.numpy as jnp
from jax import lax
from jax.sharding import Mesh, PartitionSpec as P

D = 5120
HD = 128
PAGE = 128
LIVE = 36


EPS = 1e-06
THETA = 500000.0


def rope_tables(row_count, head_width):
    half_width = head_width // 2
    frequency = THETA ** (-(jnp.arange(half_width, dtype=jnp.float32) * 2.0 / head_width))
    angles = jnp.arange(row_count, dtype=jnp.float32)[:, None] * frequency[None, :]
    return (jnp.cos(angles), jnp.sin(angles))


def rotate(heads_in, cosine, sine_table):
    half_width = heads_in.shape[-1] // 2
    leading = heads_in[..., :half_width]
    trailing = heads_in[..., half_width:]
    cos_b = cosine[:, None, :]
    sin_b = sine_table[:, None, :]
    return jnp.concatenate(
        [leading * cos_b - trailing * sin_b, trailing * cos_b + leading * sin_b], axis=-1
    )


def deal_rows(source, owner_start, owner_len, device, owners, live_rows):
    slot_count = source.shape[0]
    feature_count = source.shape[1]
    per_peer = slot_count // owners
    column = jnp.arange(per_peer, dtype=jnp.int32)[None, :]
    target_dev = jnp.arange(owners, dtype=jnp.int32)[:, None]
    my_start = owner_start[device]
    my_length = owner_len[device]
    local_index = (target_dev - my_start) % owners + owners * column
    usable = local_index < my_length
    picked = jnp.where(
        usable[:, :, None],
        source[jnp.minimum(local_index, slot_count - 1)],
        jnp.zeros((), source.dtype),
    )
    arrived = lax.all_to_all(picked, ("ra", "rb"), split_axis=0, concat_axis=0, tiled=True)
    src_start = owner_start[:, None]
    src_length = owner_len[:, None]
    sent_index = (device - src_start) % owners + owners * column
    landing = jnp.where(
        sent_index < src_length, (src_start + sent_index - device) // owners, live_rows
    )
    packed = jnp.zeros((live_rows, feature_count), source.dtype)
    return packed.at[landing.reshape(-1)].set(arrived.reshape(-1, feature_count), mode="drop")


def per_device(
    hidden_in,
    queries,
    key_proj,
    values,
    query_gain,
    key_gain,
    attn_gain,
    gate_w,
    up_w,
    lengths,
    assign,
    page_table,
):
    slot_count = hidden_in.shape[0]
    feature_count = hidden_in.shape[1]
    owners = lax.axis_size(("ra", "rb"))
    device = lax.axis_index("ra") * lax.axis_size("rb") + lax.axis_index("rb")
    head_count = feature_count // HD
    unit_count = gate_w.shape[1]
    owner_req = jnp.zeros((owners,), jnp.int32).at[assign].set(jnp.arange(owners, dtype=jnp.int32))
    starts = jnp.cumsum(lengths) - lengths
    owner_start = starts[owner_req]
    owner_len = lengths[owner_req]
    my_length = owner_len[device]
    inner_count = lax.axis_size("rb")
    own_weights = jnp.stack([gate_w, up_w])
    weights = lax.all_to_all(
        jnp.broadcast_to(own_weights[None], (inner_count,) + own_weights.shape), "rb", 0, 0, tiled=True
    )
    weights = jnp.transpose(weights, (1, 2, 0, 3)).reshape(2, own_weights.shape[1], -1)
    query_f = queries.astype(jnp.float32)
    key_f = key_proj.astype(jnp.float32)
    query_sq, key_sq = lax.psum(
        (jnp.sum(query_f * query_f, axis=1), jnp.sum(key_f * key_f, axis=1)), "wt"
    )
    query_n = query_f * lax.rsqrt(query_sq / D + EPS)[:, None] * query_gain
    key_n = key_f * lax.rsqrt(key_sq / D + EPS)[:, None] * key_gain
    cosine, sine_table = rope_tables(slot_count, HD)
    query_r = rotate(query_n.reshape(slot_count, head_count, HD), cosine, sine_table).astype(
        jnp.bfloat16
    )
    key_r = rotate(key_n.reshape(slot_count, head_count, HD), cosine, sine_table).astype(
        jnp.bfloat16
    )
    scores = jnp.einsum(
        "qhd,khd->hqk", query_r, key_r, preferred_element_type=jnp.float32
    ) * HD ** (-0.5)
    position = jnp.arange(slot_count, dtype=jnp.int32)
    allowed = (position[None, :] <= position[:, None]) & (position[None, :] < my_length)
    scores = jnp.where(allowed[None], scores, -jnp.inf)
    row_peak = jnp.max(scores, axis=2, keepdims=True)
    expd = jnp.exp(scores - row_peak)
    probabilities = (expd / jnp.sum(expd, axis=2, keepdims=True)).astype(jnp.bfloat16)
    value_heads = values.reshape(slot_count, head_count, HD)
    attended = jnp.einsum(
        "hqk,khd->qhd", probabilities, value_heads, preferred_element_type=jnp.float32
    )
    attended = attended.astype(jnp.bfloat16).reshape(slot_count, feature_count)
    attended, weights = lax.optimization_barrier((attended, weights))
    attended_f = attended.astype(jnp.float32)
    attn_sq = lax.psum(jnp.sum(attended_f * attended_f, axis=1), "wt")
    layer_rows = (
        hidden_in.astype(jnp.float32)
        + attended_f * lax.rsqrt(attn_sq / D + EPS)[:, None] * attn_gain
    ).astype(jnp.bfloat16)
    live_mask = (position < my_length)[:, None]
    page_count = slot_count // PAGE
    zero_value = jnp.zeros((), jnp.bfloat16)
    key_pages = jnp.where(live_mask, key_r.reshape(slot_count, feature_count), zero_value).reshape(
        page_count, PAGE, feature_count
    )
    value_pages = jnp.where(live_mask, values, zero_value).reshape(page_count, PAGE, feature_count)
    placement = page_table[0]
    key_cache = jnp.zeros_like(key_pages).at[placement].set(key_pages)
    value_cache = jnp.zeros_like(value_pages).at[placement].set(value_pages)
    regrouped = deal_rows(layer_rows, owner_start, owner_len, device, owners, LIVE)
    outer = lax.axis_size("ra")
    inner = lax.axis_size("rb")
    ring_pos = lax.axis_index("ra")
    ahead, behind = regrouped, regrouped
    arrived = {0: regrouped}
    for step in range(1, outer // 2 + 1):
        ahead = lax.ppermute(ahead, "ra", [(j, (j + 1) % outer) for j in range(outer)])
        arrived[step] = ahead
        if step < outer - step:
            behind = lax.ppermute(behind, "ra", [(j, (j - 1) % outer) for j in range(outer)])
            arrived[outer - step] = behind
    piece = jnp.concatenate([arrived[k] for k in range(outer)], axis=0)
    stacked = jnp.einsum("tk,skn->tsn", piece, weights, preferred_element_type=jnp.float32)
    parts = lax.axis_size("wt")
    stacked = stacked.astype(jnp.bfloat16).reshape(outer, parts, LIVE // parts, 2, inner * unit_count)
    stacked = lax.all_to_all(stacked, "wt", split_axis=1, concat_axis=1, tiled=True)
    summed = jnp.sum(stacked.astype(jnp.float32), axis=1)
    gated = (jax.nn.silu(summed[:, :, 0]) * summed[:, :, 1]).astype(jnp.bfloat16)
    rows_here = gated.shape[1]
    gated = gated.reshape(outer, rows_here, inner, unit_count)
    gated = lax.all_to_all(gated, "rb", split_axis=2, concat_axis=2, tiled=True)
    source_order = (ring_pos - jnp.arange(outer, dtype=jnp.int32)) % outer
    gated = jnp.take(gated, source_order, axis=0)
    gated = jnp.transpose(gated, (0, 2, 1, 3)).reshape(outer * inner, rows_here, unit_count)
    return (gated, key_cache, value_cache)


def solution(mesh):
    inner = 8
    outer = mesh.shape["req"] // inner
    split = Mesh(mesh.devices.reshape(outer, inner, mesh.shape["wt"]), ("ra", "rb", "wt"))
    req = ("ra", "rb")
    placed = (
        P(req, "wt"),
        P(req, "wt"),
        P(req, "wt"),
        P(req, "wt"),
        P("wt"),
        P("wt"),
        P("wt"),
        P("wt", req),
        P("wt", req),
        P(),
        P(),
        P(req, None),
    )
    return jax.shard_map(
        per_device,
        mesh=split,
        in_specs=placed,
        out_specs=(P(None, "wt", req), P(req, None, "wt"), P(req, None, "wt")),
        check_vma=False,
    )
```

```python
import jax
import jax.numpy as jnp
from jax import lax
from jax.sharding import Mesh, PartitionSpec as P

D = 5120
HD = 128
PAGE = 128
LIVE = 36


EPS = 1e-06
THETA = 500000.0


def rope_tables(row_count, head_width):
    half_width = head_width // 2
    frequency = THETA ** (-(jnp.arange(half_width, dtype=jnp.float32) * 2.0 / head_width))
    angles = jnp.arange(row_count, dtype=jnp.float32)[:, None] * frequency[None, :]
    return (jnp.cos(angles), jnp.sin(angles))


def rotate(heads_in, cosine, sine_table):
    half_width = heads_in.shape[-1] // 2
    leading = heads_in[..., :half_width]
    trailing = heads_in[..., half_width:]
    cos_b = cosine[:, None, :]
    sin_b = sine_table[:, None, :]
    return jnp.concatenate(
        [leading * cos_b - trailing * sin_b, trailing * cos_b + leading * sin_b], axis=-1
    )


def deal_rows(source, owner_start, owner_len, device, owners, live_rows):
    slot_count = source.shape[0]
    feature_count = source.shape[1]
    per_peer = slot_count // owners
    column = jnp.arange(per_peer, dtype=jnp.int32)[None, :]
    target_dev = jnp.arange(owners, dtype=jnp.int32)[:, None]
    my_start = owner_start[device]
    my_length = owner_len[device]
    local_index = (target_dev - my_start) % owners + owners * column
    usable = local_index < my_length
    picked = jnp.where(
        usable[:, :, None],
        source[jnp.minimum(local_index, slot_count - 1)],
        jnp.zeros((), source.dtype),
    )
    arrived = lax.all_to_all(picked, ("ra", "rb"), split_axis=0, concat_axis=0, tiled=True)
    src_start = owner_start[:, None]
    src_length = owner_len[:, None]
    sent_index = (device - src_start) % owners + owners * column
    landing = jnp.where(
        sent_index < src_length, (src_start + sent_index - device) // owners, live_rows
    )
    packed = jnp.zeros((live_rows, feature_count), source.dtype)
    return packed.at[landing.reshape(-1)].set(arrived.reshape(-1, feature_count), mode="drop")


def per_device(
    hidden_in,
    queries,
    key_proj,
    values,
    query_gain,
    key_gain,
    attn_gain,
    gate_w,
    up_w,
    lengths,
    assign,
    page_table,
):
    slot_count = hidden_in.shape[0]
    feature_count = hidden_in.shape[1]
    owners = lax.axis_size(("ra", "rb"))
    device = lax.axis_index("ra") * lax.axis_size("rb") + lax.axis_index("rb")
    head_count = feature_count // HD
    unit_count = gate_w.shape[1]
    owner_req = jnp.zeros((owners,), jnp.int32).at[assign].set(jnp.arange(owners, dtype=jnp.int32))
    starts = jnp.cumsum(lengths) - lengths
    owner_start = starts[owner_req]
    owner_len = lengths[owner_req]
    my_length = owner_len[device]
    weights = lax.all_gather(jnp.stack([gate_w, up_w]), "rb", axis=2, tiled=True)
    query_f = queries.astype(jnp.float32)
    key_f = key_proj.astype(jnp.float32)
    query_sq, key_sq = lax.psum(
        (jnp.sum(query_f * query_f, axis=1), jnp.sum(key_f * key_f, axis=1)), "wt"
    )
    query_n = query_f * lax.rsqrt(query_sq / D + EPS)[:, None] * query_gain
    key_n = key_f * lax.rsqrt(key_sq / D + EPS)[:, None] * key_gain
    cosine, sine_table = rope_tables(slot_count, HD)
    query_r = rotate(query_n.reshape(slot_count, head_count, HD), cosine, sine_table).astype(
        jnp.bfloat16
    )
    key_r = rotate(key_n.reshape(slot_count, head_count, HD), cosine, sine_table).astype(
        jnp.bfloat16
    )
    scores = jnp.einsum(
        "qhd,khd->hqk", query_r, key_r, preferred_element_type=jnp.float32
    ) * HD ** (-0.5)
    position = jnp.arange(slot_count, dtype=jnp.int32)
    allowed = (position[None, :] <= position[:, None]) & (position[None, :] < my_length)
    scores = jnp.where(allowed[None], scores, -jnp.inf)
    row_peak = jnp.max(scores, axis=2, keepdims=True)
    expd = jnp.exp(scores - row_peak)
    probabilities = (expd / jnp.sum(expd, axis=2, keepdims=True)).astype(jnp.bfloat16)
    value_heads = values.reshape(slot_count, head_count, HD)
    attended = jnp.einsum(
        "hqk,khd->qhd", probabilities, value_heads, preferred_element_type=jnp.float32
    )
    attended = attended.astype(jnp.bfloat16).reshape(slot_count, feature_count)
    attended_f = attended.astype(jnp.float32)
    attn_sq = lax.psum(jnp.sum(attended_f * attended_f, axis=1), "wt")
    layer_rows = (
        hidden_in.astype(jnp.float32)
        + attended_f * lax.rsqrt(attn_sq / D + EPS)[:, None] * attn_gain
    ).astype(jnp.bfloat16)
    live_mask = (position < my_length)[:, None]
    page_count = slot_count // PAGE
    zero_value = jnp.zeros((), jnp.bfloat16)
    key_pages = jnp.where(live_mask, key_r.reshape(slot_count, feature_count), zero_value).reshape(
        page_count, PAGE, feature_count
    )
    value_pages = jnp.where(live_mask, values, zero_value).reshape(page_count, PAGE, feature_count)
    placement = page_table[0]
    key_cache = jnp.zeros_like(key_pages).at[placement].set(key_pages)
    value_cache = jnp.zeros_like(value_pages).at[placement].set(value_pages)
    regrouped = deal_rows(layer_rows, owner_start, owner_len, device, owners, LIVE)
    regrouped, weights = lax.optimization_barrier((regrouped, weights))
    outer = lax.axis_size("ra")
    inner = lax.axis_size("rb")
    piece = lax.all_gather(regrouped, "ra", axis=0, tiled=True)
    stacked = jnp.einsum("tk,skn->tsn", piece, weights, preferred_element_type=jnp.float32)
    parts = lax.axis_size("wt")
    stacked = stacked.astype(jnp.bfloat16).reshape(outer, parts, LIVE // parts, 2, inner * unit_count)
    stacked = lax.all_to_all(stacked, "wt", split_axis=1, concat_axis=1, tiled=True)
    summed = jnp.sum(stacked.astype(jnp.float32), axis=1)
    gated = (jax.nn.silu(summed[:, :, 0]) * summed[:, :, 1]).astype(jnp.bfloat16)
    rows_here = gated.shape[1]
    gated = gated.reshape(outer, rows_here, inner, unit_count)
    gated = lax.all_to_all(gated, "rb", split_axis=2, concat_axis=2, tiled=True)
    gated = jnp.transpose(gated, (0, 2, 1, 3)).reshape(outer * inner, rows_here, unit_count)
    return (gated, key_cache, value_cache)


def solution(mesh):
    inner = 16
    outer = mesh.shape["req"] // inner
    split = Mesh(mesh.devices.reshape(outer, inner, mesh.shape["wt"]), ("ra", "rb", "wt"))
    req = ("ra", "rb")
    placed = (
        P(req, "wt"),
        P(req, "wt"),
        P(req, "wt"),
        P(req, "wt"),
        P("wt"),
        P("wt"),
        P("wt"),
        P("wt", req),
        P("wt", req),
        P(),
        P(),
        P(req, None),
    )
    return jax.shard_map(
        per_device,
        mesh=split,
        in_specs=placed,
        out_specs=(P(None, "wt", req), P(req, None, "wt"), P(req, None, "wt")),
        check_vma=False,
    )
```

```python
import jax
import jax.numpy as jnp
from jax import lax
from jax.sharding import Mesh, PartitionSpec as P

D = 5120
HD = 128
PAGE = 128
LIVE = 36


EPS = 1e-06
THETA = 500000.0


def rope_tables(row_count, head_width):
    half_width = head_width // 2
    frequency = THETA ** (-(jnp.arange(half_width, dtype=jnp.float32) * 2.0 / head_width))
    angles = jnp.arange(row_count, dtype=jnp.float32)[:, None] * frequency[None, :]
    return (jnp.cos(angles), jnp.sin(angles))


def rotate(heads_in, cosine, sine_table):
    half_width = heads_in.shape[-1] // 2
    leading = heads_in[..., :half_width]
    trailing = heads_in[..., half_width:]
    cos_b = cosine[:, None, :]
    sin_b = sine_table[:, None, :]
    return jnp.concatenate(
        [leading * cos_b - trailing * sin_b, trailing * cos_b + leading * sin_b], axis=-1
    )


def deal_rows(source, owner_start, owner_len, device, owners, live_rows):
    slot_count = source.shape[0]
    feature_count = source.shape[1]
    per_peer = slot_count // owners
    column = jnp.arange(per_peer, dtype=jnp.int32)[None, :]
    target_dev = jnp.arange(owners, dtype=jnp.int32)[:, None]
    my_start = owner_start[device]
    my_length = owner_len[device]
    local_index = (target_dev - my_start) % owners + owners * column
    usable = local_index < my_length
    picked = jnp.where(
        usable[:, :, None],
        source[jnp.minimum(local_index, slot_count - 1)],
        jnp.zeros((), source.dtype),
    )
    arrived = lax.all_to_all(picked, ("ra", "rb"), split_axis=0, concat_axis=0, tiled=True)
    src_start = owner_start[:, None]
    src_length = owner_len[:, None]
    sent_index = (device - src_start) % owners + owners * column
    landing = jnp.where(
        sent_index < src_length, (src_start + sent_index - device) // owners, live_rows
    )
    packed = jnp.zeros((live_rows, feature_count), source.dtype)
    return packed.at[landing.reshape(-1)].set(arrived.reshape(-1, feature_count), mode="drop")


def per_device(
    hidden_in,
    queries,
    key_proj,
    values,
    query_gain,
    key_gain,
    attn_gain,
    gate_w,
    up_w,
    lengths,
    assign,
    page_table,
):
    slot_count = hidden_in.shape[0]
    feature_count = hidden_in.shape[1]
    owners = lax.axis_size(("ra", "rb"))
    device = lax.axis_index("ra") * lax.axis_size("rb") + lax.axis_index("rb")
    head_count = feature_count // HD
    unit_count = gate_w.shape[1]
    owner_req = jnp.zeros((owners,), jnp.int32).at[assign].set(jnp.arange(owners, dtype=jnp.int32))
    starts = jnp.cumsum(lengths) - lengths
    owner_start = starts[owner_req]
    owner_len = lengths[owner_req]
    my_length = owner_len[device]
    halves = jnp.stack([gate_w, up_w]).reshape(2, 2, gate_w.shape[0] // 2, gate_w.shape[1])
    weights = lax.all_gather(halves, "rb", axis=3, tiled=True)
    query_f = queries.astype(jnp.float32)
    key_f = key_proj.astype(jnp.float32)
    query_sq, key_sq = lax.psum(
        (jnp.sum(query_f * query_f, axis=1), jnp.sum(key_f * key_f, axis=1)), "wt"
    )
    query_n = query_f * lax.rsqrt(query_sq / D + EPS)[:, None] * query_gain
    key_n = key_f * lax.rsqrt(key_sq / D + EPS)[:, None] * key_gain
    cosine, sine_table = rope_tables(slot_count, HD)
    query_r = rotate(query_n.reshape(slot_count, head_count, HD), cosine, sine_table).astype(
        jnp.bfloat16
    )
    key_r = rotate(key_n.reshape(slot_count, head_count, HD), cosine, sine_table).astype(
        jnp.bfloat16
    )
    scores = jnp.einsum(
        "qhd,khd->hqk", query_r, key_r, preferred_element_type=jnp.float32
    ) * HD ** (-0.5)
    position = jnp.arange(slot_count, dtype=jnp.int32)
    allowed = (position[None, :] <= position[:, None]) & (position[None, :] < my_length)
    scores = jnp.where(allowed[None], scores, -jnp.inf)
    row_peak = jnp.max(scores, axis=2, keepdims=True)
    expd = jnp.exp(scores - row_peak)
    probabilities = (expd / jnp.sum(expd, axis=2, keepdims=True)).astype(jnp.bfloat16)
    value_heads = values.reshape(slot_count, head_count, HD)
    attended = jnp.einsum(
        "hqk,khd->qhd", probabilities, value_heads, preferred_element_type=jnp.float32
    )
    attended = attended.astype(jnp.bfloat16).reshape(slot_count, feature_count)
    attended_f = attended.astype(jnp.float32)
    attn_sq = lax.psum(jnp.sum(attended_f * attended_f, axis=1), "wt")
    layer_rows = (
        hidden_in.astype(jnp.float32)
        + attended_f * lax.rsqrt(attn_sq / D + EPS)[:, None] * attn_gain
    ).astype(jnp.bfloat16)
    live_mask = (position < my_length)[:, None]
    page_count = slot_count // PAGE
    zero_value = jnp.zeros((), jnp.bfloat16)
    key_pages = jnp.where(live_mask, key_r.reshape(slot_count, feature_count), zero_value).reshape(
        page_count, PAGE, feature_count
    )
    value_pages = jnp.where(live_mask, values, zero_value).reshape(page_count, PAGE, feature_count)
    placement = page_table[0]
    key_cache = jnp.zeros_like(key_pages).at[placement].set(key_pages)
    value_cache = jnp.zeros_like(value_pages).at[placement].set(value_pages)
    half = feature_count // 2
    first = deal_rows(layer_rows[:, :half], owner_start, owner_len, device, owners, LIVE)
    second = deal_rows(layer_rows[:, half:], owner_start, owner_len, device, owners, LIVE)
    first, weights = lax.optimization_barrier((first, weights))
    outer = lax.axis_size("ra")
    inner = lax.axis_size("rb")
    piece_a = lax.all_gather(first, "ra", axis=0, tiled=True)
    piece_b = lax.all_gather(second, "ra", axis=0, tiled=True)
    stacked = jnp.einsum(
        "tk,skn->tsn", piece_a, weights[:, 0], preferred_element_type=jnp.float32
    ) + jnp.einsum("tk,skn->tsn", piece_b, weights[:, 1], preferred_element_type=jnp.float32)
    parts = lax.axis_size("wt")
    stacked = stacked.astype(jnp.bfloat16).reshape(outer, parts, LIVE // parts, 2, inner * unit_count)
    stacked = lax.all_to_all(stacked, "wt", split_axis=1, concat_axis=1, tiled=True)
    summed = jnp.sum(stacked.astype(jnp.float32), axis=1)
    gated = (jax.nn.silu(summed[:, :, 0]) * summed[:, :, 1]).astype(jnp.bfloat16)
    rows_here = gated.shape[1]
    gated = gated.reshape(outer, rows_here, inner, unit_count)
    gated = lax.all_to_all(gated, "rb", split_axis=2, concat_axis=2, tiled=True)
    gated = jnp.transpose(gated, (0, 2, 1, 3)).reshape(outer * inner, rows_here, unit_count)
    return (gated, key_cache, value_cache)


def solution(mesh):
    inner = 16
    outer = mesh.shape["req"] // inner
    split = Mesh(mesh.devices.reshape(outer, inner, mesh.shape["wt"]), ("ra", "rb", "wt"))
    req = ("ra", "rb")
    placed = (
        P(req, "wt"),
        P(req, "wt"),
        P(req, "wt"),
        P(req, "wt"),
        P("wt"),
        P("wt"),
        P("wt"),
        P("wt", req),
        P("wt", req),
        P(),
        P(),
        P(req, None),
    )
    return jax.shard_map(
        per_device,
        mesh=split,
        in_specs=placed,
        out_specs=(P(None, "wt", req), P(req, None, "wt"), P(req, None, "wt")),
        check_vma=False,
    )
```

```python
import jax
import jax.numpy as jnp
from jax import lax
from jax.sharding import Mesh, PartitionSpec as P

D = 5120
HD = 128
PAGE = 128
LIVE = 36


EPS = 1e-06
THETA = 500000.0


def rope_tables(row_count, head_width):
    half_width = head_width // 2
    frequency = THETA ** (-(jnp.arange(half_width, dtype=jnp.float32) * 2.0 / head_width))
    angles = jnp.arange(row_count, dtype=jnp.float32)[:, None] * frequency[None, :]
    return (jnp.cos(angles), jnp.sin(angles))


def rotate(heads_in, cosine, sine_table):
    half_width = heads_in.shape[-1] // 2
    leading = heads_in[..., :half_width]
    trailing = heads_in[..., half_width:]
    cos_b = cosine[:, None, :]
    sin_b = sine_table[:, None, :]
    return jnp.concatenate(
        [leading * cos_b - trailing * sin_b, trailing * cos_b + leading * sin_b], axis=-1
    )


def deal_rows(source, owner_start, owner_len, device, owners, live_rows):
    slot_count = source.shape[0]
    feature_count = source.shape[1]
    per_peer = slot_count // owners
    column = jnp.arange(per_peer, dtype=jnp.int32)[None, :]
    target_dev = jnp.arange(owners, dtype=jnp.int32)[:, None]
    my_start = owner_start[device]
    my_length = owner_len[device]
    local_index = (target_dev - my_start) % owners + owners * column
    usable = local_index < my_length
    picked = jnp.where(
        usable[:, :, None],
        source[jnp.minimum(local_index, slot_count - 1)],
        jnp.zeros((), source.dtype),
    )
    arrived = lax.all_to_all(picked, ("ra", "rb"), split_axis=0, concat_axis=0, tiled=True)
    src_start = owner_start[:, None]
    src_length = owner_len[:, None]
    sent_index = (device - src_start) % owners + owners * column
    landing = jnp.where(
        sent_index < src_length, (src_start + sent_index - device) // owners, live_rows
    )
    packed = jnp.zeros((live_rows, feature_count), source.dtype)
    return packed.at[landing.reshape(-1)].set(arrived.reshape(-1, feature_count), mode="drop")


def per_device(
    hidden_in,
    queries,
    key_proj,
    values,
    query_gain,
    key_gain,
    attn_gain,
    gate_w,
    up_w,
    lengths,
    assign,
    page_table,
):
    slot_count = hidden_in.shape[0]
    feature_count = hidden_in.shape[1]
    owners = lax.axis_size(("ra", "rb"))
    device = lax.axis_index("ra") * lax.axis_size("rb") + lax.axis_index("rb")
    head_count = feature_count // HD
    unit_count = gate_w.shape[1]
    owner_req = jnp.zeros((owners,), jnp.int32).at[assign].set(jnp.arange(owners, dtype=jnp.int32))
    starts = jnp.cumsum(lengths) - lengths
    owner_start = starts[owner_req]
    owner_len = lengths[owner_req]
    my_length = owner_len[device]
    weights = lax.all_gather(jnp.stack([gate_w, up_w]), "rb", axis=2, tiled=True)
    query_f = queries.astype(jnp.float32)
    key_f = key_proj.astype(jnp.float32)
    query_sq, key_sq = lax.psum(
        (jnp.sum(query_f * query_f, axis=1), jnp.sum(key_f * key_f, axis=1)), "wt"
    )
    query_n = query_f * lax.rsqrt(query_sq / D + EPS)[:, None] * query_gain
    key_n = key_f * lax.rsqrt(key_sq / D + EPS)[:, None] * key_gain
    cosine, sine_table = rope_tables(slot_count, HD)
    query_r = rotate(query_n.reshape(slot_count, head_count, HD), cosine, sine_table).astype(
        jnp.bfloat16
    )
    key_r = rotate(key_n.reshape(slot_count, head_count, HD), cosine, sine_table).astype(
        jnp.bfloat16
    )
    scores = jnp.einsum(
        "qhd,khd->hqk", query_r, key_r, preferred_element_type=jnp.float32
    ) * HD ** (-0.5)
    position = jnp.arange(slot_count, dtype=jnp.int32)
    allowed = (position[None, :] <= position[:, None]) & (position[None, :] < my_length)
    scores = jnp.where(allowed[None], scores, -jnp.inf)
    row_peak = jnp.max(scores, axis=2, keepdims=True)
    expd = jnp.exp(scores - row_peak)
    probabilities = (expd / jnp.sum(expd, axis=2, keepdims=True)).astype(jnp.bfloat16)
    value_heads = values.reshape(slot_count, head_count, HD)
    attended = jnp.einsum(
        "hqk,khd->qhd", probabilities, value_heads, preferred_element_type=jnp.float32
    )
    attended = attended.astype(jnp.bfloat16).reshape(slot_count, feature_count)
    attended_f = attended.astype(jnp.float32)
    attn_sq = lax.psum(jnp.sum(attended_f * attended_f, axis=1), "wt")
    layer_rows = (
        hidden_in.astype(jnp.float32)
        + attended_f * lax.rsqrt(attn_sq / D + EPS)[:, None] * attn_gain
    ).astype(jnp.bfloat16)
    live_mask = (position < my_length)[:, None]
    page_count = slot_count // PAGE
    zero_value = jnp.zeros((), jnp.bfloat16)
    key_pages = jnp.where(live_mask, key_r.reshape(slot_count, feature_count), zero_value).reshape(
        page_count, PAGE, feature_count
    )
    value_pages = jnp.where(live_mask, values, zero_value).reshape(page_count, PAGE, feature_count)
    placement = page_table[0]
    key_cache = jnp.zeros_like(key_pages).at[placement].set(key_pages)
    value_cache = jnp.zeros_like(value_pages).at[placement].set(value_pages)
    regrouped = deal_rows(layer_rows, owner_start, owner_len, device, owners, LIVE)
    regrouped, weights = lax.optimization_barrier((regrouped, weights))
    outer = lax.axis_size("ra")
    inner = lax.axis_size("rb")
    piece = lax.all_gather(regrouped, "ra", axis=0, tiled=True)
    stacked = jnp.einsum("tk,skn->tsn", piece, weights, preferred_element_type=jnp.float32)
    parts = lax.axis_size("wt")
    rows_here = LIVE // parts
    stacked = stacked.astype(jnp.bfloat16).reshape(outer, parts, rows_here, 2, inner, unit_count)
    stacked = jnp.transpose(stacked, (4, 1, 0, 2, 3, 5)).reshape(
        inner * parts, outer, rows_here, 2, unit_count
    )
    stacked = lax.all_to_all(stacked, ("rb", "wt"), split_axis=0, concat_axis=0, tiled=True)
    stacked = stacked.reshape(inner, parts, outer, rows_here, 2, unit_count)
    summed = jnp.sum(stacked.astype(jnp.float32), axis=1)
    gated = (jax.nn.silu(summed[:, :, :, 0]) * summed[:, :, :, 1]).astype(jnp.bfloat16)
    gated = jnp.transpose(gated, (1, 0, 2, 3)).reshape(outer * inner, rows_here, unit_count)
    return (gated, key_cache, value_cache)


def solution(mesh):
    inner = 16
    outer = mesh.shape["req"] // inner
    split = Mesh(mesh.devices.reshape(outer, inner, mesh.shape["wt"]), ("ra", "rb", "wt"))
    req = ("ra", "rb")
    placed = (
        P(req, "wt"),
        P(req, "wt"),
        P(req, "wt"),
        P(req, "wt"),
        P("wt"),
        P("wt"),
        P("wt"),
        P("wt", req),
        P("wt", req),
        P(),
        P(),
        P(req, None),
    )
    return jax.shard_map(
        per_device,
        mesh=split,
        in_specs=placed,
        out_specs=(P(None, "wt", req), P(req, None, "wt"), P(req, None, "wt")),
        check_vma=False,
    )
```

```python
import jax
import jax.numpy as jnp
from jax import lax
from jax.sharding import Mesh, PartitionSpec as P

D = 5120
HD = 128
PAGE = 128
LIVE = 36


EPS = 1e-06
THETA = 500000.0


def rope_tables(row_count, head_width):
    half_width = head_width // 2
    frequency = THETA ** (-(jnp.arange(half_width, dtype=jnp.float32) * 2.0 / head_width))
    angles = jnp.arange(row_count, dtype=jnp.float32)[:, None] * frequency[None, :]
    return (jnp.cos(angles), jnp.sin(angles))


def rotate(heads_in, cosine, sine_table):
    half_width = heads_in.shape[-1] // 2
    leading = heads_in[..., :half_width]
    trailing = heads_in[..., half_width:]
    cos_b = cosine[:, None, :]
    sin_b = sine_table[:, None, :]
    return jnp.concatenate(
        [leading * cos_b - trailing * sin_b, trailing * cos_b + leading * sin_b], axis=-1
    )


def deal_rows(source, owner_start, owner_len, device, owners, live_rows):
    slot_count = source.shape[0]
    feature_count = source.shape[1]
    per_peer = slot_count // owners
    column = jnp.arange(per_peer, dtype=jnp.int32)[None, :]
    target_dev = jnp.arange(owners, dtype=jnp.int32)[:, None]
    my_start = owner_start[device]
    my_length = owner_len[device]
    local_index = (target_dev - my_start) % owners + owners * column
    usable = local_index < my_length
    picked = jnp.where(
        usable[:, :, None],
        source[jnp.minimum(local_index, slot_count - 1)],
        jnp.zeros((), source.dtype),
    )
    arrived = lax.all_to_all(picked, ("ra", "rb"), split_axis=0, concat_axis=0, tiled=True)
    src_start = owner_start[:, None]
    src_length = owner_len[:, None]
    sent_index = (device - src_start) % owners + owners * column
    landing = jnp.where(
        sent_index < src_length, (src_start + sent_index - device) // owners, live_rows
    )
    packed = jnp.zeros((live_rows, feature_count), source.dtype)
    return packed.at[landing.reshape(-1)].set(arrived.reshape(-1, feature_count), mode="drop")


def per_device(
    hidden_in,
    queries,
    key_proj,
    values,
    query_gain,
    key_gain,
    attn_gain,
    gate_w,
    up_w,
    lengths,
    assign,
    page_table,
):
    slot_count = hidden_in.shape[0]
    feature_count = hidden_in.shape[1]
    owners = lax.axis_size(("ra", "rb"))
    device = lax.axis_index("ra") * lax.axis_size("rb") + lax.axis_index("rb")
    head_count = feature_count // HD
    unit_count = gate_w.shape[1]
    owner_req = jnp.zeros((owners,), jnp.int32).at[assign].set(jnp.arange(owners, dtype=jnp.int32))
    starts = jnp.cumsum(lengths) - lengths
    owner_start = starts[owner_req]
    owner_len = lengths[owner_req]
    my_length = owner_len[device]
    weights = lax.all_gather(jnp.stack([gate_w, up_w]), "rb", axis=2, tiled=True)
    query_f = queries.astype(jnp.float32)
    key_f = key_proj.astype(jnp.float32)
    query_sq, key_sq = lax.psum(
        (jnp.sum(query_f * query_f, axis=1), jnp.sum(key_f * key_f, axis=1)), "wt"
    )
    query_n = query_f * lax.rsqrt(query_sq / D + EPS)[:, None] * query_gain
    key_n = key_f * lax.rsqrt(key_sq / D + EPS)[:, None] * key_gain
    cosine, sine_table = rope_tables(slot_count, HD)
    query_r = rotate(query_n.reshape(slot_count, head_count, HD), cosine, sine_table).astype(
        jnp.bfloat16
    )
    key_r = rotate(key_n.reshape(slot_count, head_count, HD), cosine, sine_table).astype(
        jnp.bfloat16
    )
    scores = jnp.einsum(
        "qhd,khd->hqk", query_r, key_r, preferred_element_type=jnp.float32
    ) * HD ** (-0.5)
    position = jnp.arange(slot_count, dtype=jnp.int32)
    allowed = (position[None, :] <= position[:, None]) & (position[None, :] < my_length)
    scores = jnp.where(allowed[None], scores, -jnp.inf)
    row_peak = jnp.max(scores, axis=2, keepdims=True)
    expd = jnp.exp(scores - row_peak)
    probabilities = (expd / jnp.sum(expd, axis=2, keepdims=True)).astype(jnp.bfloat16)
    value_heads = values.reshape(slot_count, head_count, HD)
    attended = jnp.einsum(
        "hqk,khd->qhd", probabilities, value_heads, preferred_element_type=jnp.float32
    )
    attended = attended.astype(jnp.bfloat16).reshape(slot_count, feature_count)
    attended_f = attended.astype(jnp.float32)
    attn_sq = lax.psum(jnp.sum(attended_f * attended_f, axis=1), "wt")
    layer_rows = (
        hidden_in.astype(jnp.float32)
        + attended_f * lax.rsqrt(attn_sq / D + EPS)[:, None] * attn_gain
    ).astype(jnp.bfloat16)
    live_mask = (position < my_length)[:, None]
    page_count = slot_count // PAGE
    zero_value = jnp.zeros((), jnp.bfloat16)
    key_pages = jnp.where(live_mask, key_r.reshape(slot_count, feature_count), zero_value).reshape(
        page_count, PAGE, feature_count
    )
    value_pages = jnp.where(live_mask, values, zero_value).reshape(page_count, PAGE, feature_count)
    placement = page_table[0]
    key_cache = jnp.zeros_like(key_pages).at[placement].set(key_pages)
    value_cache = jnp.zeros_like(value_pages).at[placement].set(value_pages)
    regrouped = deal_rows(layer_rows, owner_start, owner_len, device, owners, LIVE)
    regrouped, weights = lax.optimization_barrier((regrouped, weights))
    outer = lax.axis_size("ra")
    inner = lax.axis_size("rb")
    piece = lax.all_gather(regrouped, "ra", axis=0, tiled=True)
    parts = lax.axis_size("wt")
    piece = jnp.transpose(piece.reshape(outer, parts, LIVE // parts, feature_count), (1, 0, 2, 3))
    stacked = jnp.einsum("wrtk,skn->wrtsn", piece, weights, preferred_element_type=jnp.float32)
    stacked = lax.all_to_all(stacked.astype(jnp.bfloat16), "wt", split_axis=0, concat_axis=0, tiled=True)
    summed = jnp.sum(stacked.astype(jnp.float32), axis=0)
    gated = (jax.nn.silu(summed[:, :, 0]) * summed[:, :, 1]).astype(jnp.bfloat16)
    rows_here = gated.shape[1]
    gated = gated.reshape(outer, rows_here, inner, unit_count)
    gated = lax.all_to_all(gated, "rb", split_axis=2, concat_axis=2, tiled=True)
    gated = jnp.transpose(gated, (0, 2, 1, 3)).reshape(outer * inner, rows_here, unit_count)
    return (gated, key_cache, value_cache)


def solution(mesh):
    inner = 16
    outer = mesh.shape["req"] // inner
    split = Mesh(mesh.devices.reshape(outer, inner, mesh.shape["wt"]), ("ra", "rb", "wt"))
    req = ("ra", "rb")
    placed = (
        P(req, "wt"),
        P(req, "wt"),
        P(req, "wt"),
        P(req, "wt"),
        P("wt"),
        P("wt"),
        P("wt"),
        P("wt", req),
        P("wt", req),
        P(),
        P(),
        P(req, None),
    )
    return jax.shard_map(
        per_device,
        mesh=split,
        in_specs=placed,
        out_specs=(P(None, "wt", req), P(req, None, "wt"), P(req, None, "wt")),
        check_vma=False,
    )
```

```python
import jax
import jax.numpy as jnp
from jax import lax
from jax.sharding import Mesh, PartitionSpec as P

D = 5120
HD = 128
PAGE = 128
LIVE = 36


EPS = 1e-06
THETA = 500000.0


def rope_tables(row_count, head_width):
    half_width = head_width // 2
    frequency = THETA ** (-(jnp.arange(half_width, dtype=jnp.float32) * 2.0 / head_width))
    angles = jnp.arange(row_count, dtype=jnp.float32)[:, None] * frequency[None, :]
    return (jnp.cos(angles), jnp.sin(angles))


def rotate(heads_in, cosine, sine_table):
    half_width = heads_in.shape[-1] // 2
    leading = heads_in[..., :half_width]
    trailing = heads_in[..., half_width:]
    cos_b = cosine[:, None, :]
    sin_b = sine_table[:, None, :]
    return jnp.concatenate(
        [leading * cos_b - trailing * sin_b, trailing * cos_b + leading * sin_b], axis=-1
    )


def deal_rows(source, owner_start, owner_len, device, owners, live_rows):
    slot_count = source.shape[0]
    feature_count = source.shape[1]
    per_peer = slot_count // owners
    column = jnp.arange(per_peer, dtype=jnp.int32)[None, :]
    target_dev = jnp.arange(owners, dtype=jnp.int32)[:, None]
    my_start = owner_start[device]
    my_length = owner_len[device]
    local_index = (target_dev - my_start) % owners + owners * column
    usable = local_index < my_length
    picked = jnp.where(
        usable[:, :, None],
        source[jnp.minimum(local_index, slot_count - 1)],
        jnp.zeros((), source.dtype),
    )
    arrived = lax.all_to_all(picked, ("ra", "rb"), split_axis=0, concat_axis=0, tiled=True)
    src_start = owner_start[:, None]
    src_length = owner_len[:, None]
    sent_index = (device - src_start) % owners + owners * column
    landing = jnp.where(
        sent_index < src_length, (src_start + sent_index - device) // owners, live_rows
    )
    packed = jnp.zeros((live_rows, feature_count), source.dtype)
    return packed.at[landing.reshape(-1)].set(arrived.reshape(-1, feature_count), mode="drop")


def per_device(
    hidden_in,
    queries,
    key_proj,
    values,
    query_gain,
    key_gain,
    attn_gain,
    gate_w,
    up_w,
    lengths,
    assign,
    page_table,
):
    slot_count = hidden_in.shape[0]
    feature_count = hidden_in.shape[1]
    owners = lax.axis_size(("ra", "rb"))
    device = lax.axis_index("ra") * lax.axis_size("rb") + lax.axis_index("rb")
    head_count = feature_count // HD
    unit_count = gate_w.shape[1]
    owner_req = jnp.zeros((owners,), jnp.int32).at[assign].set(jnp.arange(owners, dtype=jnp.int32))
    starts = jnp.cumsum(lengths) - lengths
    owner_start = starts[owner_req]
    owner_len = lengths[owner_req]
    my_length = owner_len[device]
    weights = lax.all_gather(jnp.stack([gate_w, up_w]), "rb", axis=2, tiled=True)
    query_f = queries.astype(jnp.float32)
    key_f = key_proj.astype(jnp.float32)
    query_sq, key_sq = lax.psum(
        (jnp.sum(query_f * query_f, axis=1), jnp.sum(key_f * key_f, axis=1)), "wt"
    )
    query_n = query_f * lax.rsqrt(query_sq / D + EPS)[:, None] * query_gain
    key_n = key_f * lax.rsqrt(key_sq / D + EPS)[:, None] * key_gain
    cosine, sine_table = rope_tables(slot_count, HD)
    query_r = rotate(query_n.reshape(slot_count, head_count, HD), cosine, sine_table).astype(
        jnp.bfloat16
    )
    key_r = rotate(key_n.reshape(slot_count, head_count, HD), cosine, sine_table).astype(
        jnp.bfloat16
    )
    scores = jnp.einsum(
        "qhd,khd->hqk", query_r, key_r, preferred_element_type=jnp.float32
    ) * HD ** (-0.5)
    position = jnp.arange(slot_count, dtype=jnp.int32)
    allowed = (position[None, :] <= position[:, None]) & (position[None, :] < my_length)
    scores = jnp.where(allowed[None], scores, -jnp.inf)
    row_peak = jnp.max(scores, axis=2, keepdims=True)
    expd = jnp.exp(scores - row_peak)
    probabilities = (expd / jnp.sum(expd, axis=2, keepdims=True)).astype(jnp.bfloat16)
    value_heads = values.reshape(slot_count, head_count, HD)
    attended = jnp.einsum(
        "hqk,khd->qhd", probabilities, value_heads, preferred_element_type=jnp.float32
    )
    attended = attended.astype(jnp.bfloat16).reshape(slot_count, feature_count)
    attended_f = attended.astype(jnp.float32)
    attn_sq = lax.psum(jnp.sum(attended_f * attended_f, axis=1), "wt")
    layer_rows = (
        hidden_in.astype(jnp.float32)
        + attended_f * lax.rsqrt(attn_sq / D + EPS)[:, None] * attn_gain
    ).astype(jnp.bfloat16)
    live_mask = (position < my_length)[:, None]
    page_count = slot_count // PAGE
    zero_value = jnp.zeros((), jnp.bfloat16)
    key_pages = jnp.where(live_mask, key_r.reshape(slot_count, feature_count), zero_value).reshape(
        page_count, PAGE, feature_count
    )
    value_pages = jnp.where(live_mask, values, zero_value).reshape(page_count, PAGE, feature_count)
    placement = page_table[0]
    key_cache = jnp.zeros_like(key_pages).at[placement].set(key_pages)
    value_cache = jnp.zeros_like(value_pages).at[placement].set(value_pages)
    regrouped = deal_rows(layer_rows, owner_start, owner_len, device, owners, LIVE)
    regrouped, weights = lax.optimization_barrier((regrouped, weights))
    outer = lax.axis_size("ra")
    inner = lax.axis_size("rb")
    piece = lax.all_to_all(
        jnp.broadcast_to(regrouped[None], (outer,) + regrouped.shape), "ra", 0, 0, tiled=True
    )
    parts = lax.axis_size("wt")
    piece = jnp.transpose(piece.reshape(outer, parts, LIVE // parts, feature_count), (1, 0, 2, 3))
    stacked = jnp.einsum("wrtk,skn->wrtsn", piece, weights, preferred_element_type=jnp.float32)
    stacked = lax.all_to_all(stacked.astype(jnp.bfloat16), "wt", split_axis=0, concat_axis=0, tiled=True)
    summed = jnp.sum(stacked.astype(jnp.float32), axis=0)
    gated = (jax.nn.silu(summed[:, :, 0]) * summed[:, :, 1]).astype(jnp.bfloat16)
    rows_here = gated.shape[1]
    gated = gated.reshape(outer, rows_here, inner, unit_count)
    gated = lax.all_to_all(gated, "rb", split_axis=2, concat_axis=2, tiled=True)
    gated = jnp.transpose(gated, (0, 2, 1, 3)).reshape(outer * inner, rows_here, unit_count)
    return (gated, key_cache, value_cache)


def solution(mesh):
    inner = 16
    outer = mesh.shape["req"] // inner
    split = Mesh(mesh.devices.reshape(outer, inner, mesh.shape["wt"]), ("ra", "rb", "wt"))
    req = ("ra", "rb")
    placed = (
        P(req, "wt"),
        P(req, "wt"),
        P(req, "wt"),
        P(req, "wt"),
        P("wt"),
        P("wt"),
        P("wt"),
        P("wt", req),
        P("wt", req),
        P(),
        P(),
        P(req, None),
    )
    return jax.shard_map(
        per_device,
        mesh=split,
        in_specs=placed,
        out_specs=(P(None, "wt", req), P(req, None, "wt"), P(req, None, "wt")),
        check_vma=False,
    )
```

```python
import jax
import jax.numpy as jnp
from jax import lax
from jax.sharding import Mesh, PartitionSpec as P

D = 5120
HD = 128
PAGE = 128
LIVE = 36


EPS = 1e-06
THETA = 500000.0


def rope_tables(row_count, head_width):
    half_width = head_width // 2
    frequency = THETA ** (-(jnp.arange(half_width, dtype=jnp.float32) * 2.0 / head_width))
    angles = jnp.arange(row_count, dtype=jnp.float32)[:, None] * frequency[None, :]
    return (jnp.cos(angles), jnp.sin(angles))


def rotate(heads_in, cosine, sine_table):
    half_width = heads_in.shape[-1] // 2
    swapped = jnp.concatenate([heads_in[..., half_width:], heads_in[..., :half_width]], axis=-1)
    cos_full = jnp.concatenate([cosine, cosine], axis=-1)[:, None, :]
    sin_signed = jnp.concatenate([-sine_table, sine_table], axis=-1)[:, None, :]
    return heads_in * cos_full + swapped * sin_signed


def deal_rows(source, owner_start, owner_len, device, owners, live_rows):
    slot_count = source.shape[0]
    feature_count = source.shape[1]
    per_peer = slot_count // owners
    column = jnp.arange(per_peer, dtype=jnp.int32)[None, :]
    target_dev = jnp.arange(owners, dtype=jnp.int32)[:, None]
    my_start = owner_start[device]
    my_length = owner_len[device]
    local_index = (target_dev - my_start) % owners + owners * column
    usable = local_index < my_length
    picked = jnp.where(
        usable[:, :, None],
        source[jnp.minimum(local_index, slot_count - 1)],
        jnp.zeros((), source.dtype),
    )
    arrived = lax.all_to_all(picked, ("ra", "rb"), split_axis=0, concat_axis=0, tiled=True)
    src_start = owner_start[:, None]
    src_length = owner_len[:, None]
    sent_index = (device - src_start) % owners + owners * column
    landing = jnp.where(
        sent_index < src_length, (src_start + sent_index - device) // owners, live_rows
    )
    packed = jnp.zeros((live_rows, feature_count), source.dtype)
    return packed.at[landing.reshape(-1)].set(arrived.reshape(-1, feature_count), mode="drop")


def per_device(
    hidden_in,
    queries,
    key_proj,
    values,
    query_gain,
    key_gain,
    attn_gain,
    gate_w,
    up_w,
    lengths,
    assign,
    page_table,
):
    slot_count = hidden_in.shape[0]
    feature_count = hidden_in.shape[1]
    owners = lax.axis_size(("ra", "rb"))
    device = lax.axis_index("ra") * lax.axis_size("rb") + lax.axis_index("rb")
    head_count = feature_count // HD
    unit_count = gate_w.shape[1]
    owner_req = jnp.zeros((owners,), jnp.int32).at[assign].set(jnp.arange(owners, dtype=jnp.int32))
    starts = jnp.cumsum(lengths) - lengths
    owner_start = starts[owner_req]
    owner_len = lengths[owner_req]
    my_length = owner_len[device]
    weights = lax.all_gather(jnp.stack([gate_w, up_w]), "rb", axis=2, tiled=True)
    query_f = queries.astype(jnp.float32)
    key_f = key_proj.astype(jnp.float32)
    query_sq, key_sq = lax.psum(
        (jnp.sum(query_f * query_f, axis=1), jnp.sum(key_f * key_f, axis=1)), "wt"
    )
    query_n = query_f * lax.rsqrt(query_sq / D + EPS)[:, None] * query_gain
    key_n = key_f * lax.rsqrt(key_sq / D + EPS)[:, None] * key_gain
    cosine, sine_table = rope_tables(slot_count, HD)
    query_r = rotate(query_n.reshape(slot_count, head_count, HD), cosine, sine_table).astype(
        jnp.bfloat16
    )
    key_r = rotate(key_n.reshape(slot_count, head_count, HD), cosine, sine_table).astype(
        jnp.bfloat16
    )
    scores = jnp.einsum(
        "qhd,khd->hqk", query_r, key_r, preferred_element_type=jnp.float32
    ) * HD ** (-0.5)
    position = jnp.arange(slot_count, dtype=jnp.int32)
    allowed = (position[None, :] <= position[:, None]) & (position[None, :] < my_length)
    scores = jnp.where(allowed[None], scores, -jnp.inf)
    row_peak = jnp.max(scores, axis=2, keepdims=True)
    expd = jnp.exp(scores - row_peak)
    probabilities = (expd / jnp.sum(expd, axis=2, keepdims=True)).astype(jnp.bfloat16)
    value_heads = values.reshape(slot_count, head_count, HD)
    attended = jnp.einsum(
        "hqk,khd->qhd", probabilities, value_heads, preferred_element_type=jnp.float32
    )
    attended = attended.astype(jnp.bfloat16).reshape(slot_count, feature_count)
    attended_f = attended.astype(jnp.float32)
    attn_sq = lax.psum(jnp.sum(attended_f * attended_f, axis=1), "wt")
    layer_rows = (
        hidden_in.astype(jnp.float32)
        + attended_f * lax.rsqrt(attn_sq / D + EPS)[:, None] * attn_gain
    ).astype(jnp.bfloat16)
    live_mask = (position < my_length)[:, None]
    page_count = slot_count // PAGE
    zero_value = jnp.zeros((), jnp.bfloat16)
    key_pages = jnp.where(live_mask, key_r.reshape(slot_count, feature_count), zero_value).reshape(
        page_count, PAGE, feature_count
    )
    value_pages = jnp.where(live_mask, values, zero_value).reshape(page_count, PAGE, feature_count)
    placement = page_table[0]
    key_cache = jnp.zeros_like(key_pages).at[placement].set(key_pages)
    value_cache = jnp.zeros_like(value_pages).at[placement].set(value_pages)
    regrouped = deal_rows(layer_rows, owner_start, owner_len, device, owners, LIVE)
    regrouped, weights = lax.optimization_barrier((regrouped, weights))
    outer = lax.axis_size("ra")
    inner = lax.axis_size("rb")
    piece = lax.all_gather(regrouped, "ra", axis=0, tiled=True)
    parts = lax.axis_size("wt")
    piece = jnp.transpose(piece.reshape(outer, parts, LIVE // parts, feature_count), (1, 0, 2, 3))
    stacked = jnp.einsum("wrtk,skn->wrtsn", piece, weights, preferred_element_type=jnp.float32)
    stacked = lax.all_to_all(stacked.astype(jnp.bfloat16), "wt", split_axis=0, concat_axis=0, tiled=True)
    summed = jnp.sum(stacked.astype(jnp.float32), axis=0)
    gated = (jax.nn.silu(summed[:, :, 0]) * summed[:, :, 1]).astype(jnp.bfloat16)
    rows_here = gated.shape[1]
    gated = gated.reshape(outer, rows_here, inner, unit_count)
    gated = lax.all_to_all(gated, "rb", split_axis=2, concat_axis=2, tiled=True)
    gated = jnp.transpose(gated, (0, 2, 1, 3)).reshape(outer * inner, rows_here, unit_count)
    return (gated, key_cache, value_cache)


def solution(mesh):
    inner = 16
    outer = mesh.shape["req"] // inner
    split = Mesh(mesh.devices.reshape(outer, inner, mesh.shape["wt"]), ("ra", "rb", "wt"))
    req = ("ra", "rb")
    placed = (
        P(req, "wt"),
        P(req, "wt"),
        P(req, "wt"),
        P(req, "wt"),
        P("wt"),
        P("wt"),
        P("wt"),
        P("wt", req),
        P("wt", req),
        P(),
        P(),
        P(req, None),
    )
    return jax.shard_map(
        per_device,
        mesh=split,
        in_specs=placed,
        out_specs=(P(None, "wt", req), P(req, None, "wt"), P(req, None, "wt")),
        check_vma=False,
    )
```

```python
import jax
import jax.numpy as jnp
from jax import lax
from jax.sharding import Mesh, PartitionSpec as P

D = 5120
HD = 128
PAGE = 128
LIVE = 36


EPS = 1e-06
THETA = 500000.0


def rope_tables(row_count, head_width):
    half_width = head_width // 2
    frequency = THETA ** (-(jnp.arange(half_width, dtype=jnp.float32) * 2.0 / head_width))
    angles = jnp.arange(row_count, dtype=jnp.float32)[:, None] * frequency[None, :]
    return (jnp.cos(angles), jnp.sin(angles))


def rotate(heads_in, cosine, sine_table):
    half_width = heads_in.shape[-1] // 2
    leading = heads_in[..., :half_width]
    trailing = heads_in[..., half_width:]
    cos_b = cosine[:, None, :]
    sin_b = sine_table[:, None, :]
    return jnp.concatenate(
        [leading * cos_b - trailing * sin_b, trailing * cos_b + leading * sin_b], axis=-1
    )


def deal_rows(source, owner_start, owner_len, device, owners, live_rows):
    slot_count = source.shape[0]
    feature_count = source.shape[1]
    per_peer = slot_count // owners
    column = jnp.arange(per_peer, dtype=jnp.int32)[None, :]
    target_dev = jnp.arange(owners, dtype=jnp.int32)[:, None]
    my_start = owner_start[device]
    my_length = owner_len[device]
    local_index = (target_dev - my_start) % owners + owners * column
    usable = local_index < my_length
    picked = jnp.where(
        usable[:, :, None],
        source[jnp.minimum(local_index, slot_count - 1)],
        jnp.zeros((), source.dtype),
    )
    arrived = lax.all_to_all(picked, ("ra", "rb"), split_axis=0, concat_axis=0, tiled=True)
    src_start = owner_start[:, None]
    src_length = owner_len[:, None]
    sent_index = (device - src_start) % owners + owners * column
    landing = jnp.where(
        sent_index < src_length, (src_start + sent_index - device) // owners, live_rows
    )
    packed = jnp.zeros((live_rows, feature_count), source.dtype)
    return packed.at[landing.reshape(-1)].set(arrived.reshape(-1, feature_count), mode="drop")


def per_device(
    hidden_in,
    queries,
    key_proj,
    values,
    query_gain,
    key_gain,
    attn_gain,
    gate_w,
    up_w,
    lengths,
    assign,
    page_table,
):
    slot_count = hidden_in.shape[0]
    feature_count = hidden_in.shape[1]
    owners = lax.axis_size(("ra", "rb"))
    device = lax.axis_index("ra") * lax.axis_size("rb") + lax.axis_index("rb")
    head_count = feature_count // HD
    unit_count = gate_w.shape[1]
    owner_req = jnp.zeros((owners,), jnp.int32).at[assign].set(jnp.arange(owners, dtype=jnp.int32))
    starts = jnp.cumsum(lengths) - lengths
    owner_start = starts[owner_req]
    owner_len = lengths[owner_req]
    my_length = owner_len[device]
    weights = lax.all_gather(jnp.stack([gate_w, up_w]), "rb", axis=2, tiled=True)
    query_f = queries.astype(jnp.float32)
    key_f = key_proj.astype(jnp.float32)
    query_sq, key_sq = lax.psum(
        (jnp.sum(query_f * query_f, axis=1), jnp.sum(key_f * key_f, axis=1)), "wt"
    )
    query_n = query_f * lax.rsqrt(query_sq / D + EPS)[:, None] * query_gain
    key_n = key_f * lax.rsqrt(key_sq / D + EPS)[:, None] * key_gain
    cosine, sine_table = rope_tables(slot_count, HD)
    query_r = rotate(query_n.reshape(slot_count, head_count, HD), cosine, sine_table).astype(
        jnp.bfloat16
    )
    key_r = rotate(key_n.reshape(slot_count, head_count, HD), cosine, sine_table).astype(
        jnp.bfloat16
    )
    scores = jnp.einsum(
        "qhd,khd->hqk", query_r, key_r, preferred_element_type=jnp.float32
    ) * HD ** (-0.5)
    position = jnp.arange(slot_count, dtype=jnp.int32)
    allowed = (position[None, :] <= position[:, None]) & (position[None, :] < my_length)
    scores = jnp.where(allowed[None], scores, -jnp.inf)
    row_peak = jnp.max(scores, axis=2, keepdims=True)
    expd = jnp.exp(scores - row_peak)
    probabilities = (expd / jnp.sum(expd, axis=2, keepdims=True)).astype(jnp.bfloat16)
    value_heads = values.reshape(slot_count, head_count, HD)
    attended = jnp.einsum(
        "hqk,khd->qhd", probabilities, value_heads, preferred_element_type=jnp.float32
    )
    attended = attended.astype(jnp.bfloat16).reshape(slot_count, feature_count)
    attended_f = attended.astype(jnp.float32)
    attn_sq = lax.psum(jnp.sum(attended_f * attended_f, axis=1), "wt")
    layer_rows = (
        hidden_in.astype(jnp.float32)
        + attended_f * lax.rsqrt(attn_sq / D + EPS)[:, None] * attn_gain
    ).astype(jnp.bfloat16)
    live_mask = (position < my_length)[:, None]
    page_count = slot_count // PAGE
    zero_value = jnp.zeros((), jnp.bfloat16)
    key_pages = jnp.where(live_mask, key_r.reshape(slot_count, feature_count), zero_value).reshape(
        page_count, PAGE, feature_count
    )
    value_pages = jnp.where(live_mask, values, zero_value).reshape(page_count, PAGE, feature_count)
    placement = page_table[0]
    key_cache = jnp.zeros_like(key_pages).at[placement].set(key_pages)
    value_cache = jnp.zeros_like(value_pages).at[placement].set(value_pages)
    regrouped = deal_rows(layer_rows, owner_start, owner_len, device, owners, LIVE)

    outer = lax.axis_size("ra")
    inner = lax.axis_size("rb")
    piece = lax.all_gather(regrouped, "ra", axis=0, tiled=True)
    parts = lax.axis_size("wt")
    piece = jnp.transpose(piece.reshape(outer, parts, LIVE // parts, feature_count), (1, 0, 2, 3))
    stacked = jnp.einsum("wrtk,skn->wrtsn", piece, weights, preferred_element_type=jnp.float32)
    stacked = lax.all_to_all(stacked.astype(jnp.bfloat16), "wt", split_axis=0, concat_axis=0, tiled=True)
    summed = jnp.sum(stacked.astype(jnp.float32), axis=0)
    gated = (jax.nn.silu(summed[:, :, 0]) * summed[:, :, 1]).astype(jnp.bfloat16)
    rows_here = gated.shape[1]
    gated = gated.reshape(outer, rows_here, inner, unit_count)
    gated = lax.all_to_all(gated, "rb", split_axis=2, concat_axis=2, tiled=True)
    gated = jnp.transpose(gated, (0, 2, 1, 3)).reshape(outer * inner, rows_here, unit_count)
    return (gated, key_cache, value_cache)


def solution(mesh):
    inner = 16
    outer = mesh.shape["req"] // inner
    split = Mesh(mesh.devices.reshape(outer, inner, mesh.shape["wt"]), ("ra", "rb", "wt"))
    req = ("ra", "rb")
    placed = (
        P(req, "wt"),
        P(req, "wt"),
        P(req, "wt"),
        P(req, "wt"),
        P("wt"),
        P("wt"),
        P("wt"),
        P("wt", req),
        P("wt", req),
        P(),
        P(),
        P(req, None),
    )
    return jax.shard_map(
        per_device,
        mesh=split,
        in_specs=placed,
        out_specs=(P(None, "wt", req), P(req, None, "wt"), P(req, None, "wt")),
        check_vma=False,
    )
```

```python
import jax
import jax.numpy as jnp
from jax import lax
from jax.sharding import Mesh, PartitionSpec as P

D = 5120
HD = 128
PAGE = 128
LIVE = 36


EPS = 1e-06
THETA = 500000.0


def rope_tables(row_count, head_width):
    half_width = head_width // 2
    frequency = THETA ** (-(jnp.arange(half_width, dtype=jnp.float32) * 2.0 / head_width))
    angles = jnp.arange(row_count, dtype=jnp.float32)[:, None] * frequency[None, :]
    return (jnp.cos(angles), jnp.sin(angles))


def rotate(heads_in, cosine, sine_table):
    half_width = heads_in.shape[-1] // 2
    leading = heads_in[..., :half_width]
    trailing = heads_in[..., half_width:]
    cos_b = cosine[:, None, :]
    sin_b = sine_table[:, None, :]
    return jnp.concatenate(
        [leading * cos_b - trailing * sin_b, trailing * cos_b + leading * sin_b], axis=-1
    )


def deal_rows(source, owner_start, owner_len, device, owners, live_rows):
    slot_count = source.shape[0]
    feature_count = source.shape[1]
    per_peer = slot_count // owners
    column = jnp.arange(per_peer, dtype=jnp.int32)[None, :]
    target_dev = jnp.arange(owners, dtype=jnp.int32)[:, None]
    my_start = owner_start[device]
    my_length = owner_len[device]
    local_index = (target_dev - my_start) % owners + owners * column
    usable = local_index < my_length
    picked = jnp.where(
        usable[:, :, None],
        source[jnp.minimum(local_index, slot_count - 1)],
        jnp.zeros((), source.dtype),
    )
    arrived = lax.all_to_all(picked, ("ra", "rb"), split_axis=0, concat_axis=0, tiled=True)
    src_start = owner_start[:, None]
    src_length = owner_len[:, None]
    sent_index = (device - src_start) % owners + owners * column
    landing = jnp.where(
        sent_index < src_length, (src_start + sent_index - device) // owners, live_rows
    )
    packed = jnp.zeros((live_rows, feature_count), source.dtype)
    return packed.at[landing.reshape(-1)].set(arrived.reshape(-1, feature_count), mode="drop")


def per_device(
    hidden_in,
    queries,
    key_proj,
    values,
    query_gain,
    key_gain,
    attn_gain,
    gate_w,
    up_w,
    lengths,
    assign,
    page_table,
):
    slot_count = hidden_in.shape[0]
    feature_count = hidden_in.shape[1]
    owners = lax.axis_size(("ra", "rb"))
    device = lax.axis_index("ra") * lax.axis_size("rb") + lax.axis_index("rb")
    head_count = feature_count // HD
    unit_count = gate_w.shape[1]
    owner_req = jnp.zeros((owners,), jnp.int32).at[assign].set(jnp.arange(owners, dtype=jnp.int32))
    starts = jnp.cumsum(lengths) - lengths
    owner_start = starts[owner_req]
    owner_len = lengths[owner_req]
    my_length = owner_len[device]
    weights = lax.all_gather(jnp.stack([gate_w, up_w]), "rb", axis=2, tiled=True)
    query_f = queries.astype(jnp.float32)
    key_f = key_proj.astype(jnp.float32)
    query_sq, key_sq = lax.psum(
        (jnp.sum(query_f * query_f, axis=1), jnp.sum(key_f * key_f, axis=1)), "wt"
    )
    query_n = query_f * lax.rsqrt(query_sq / D + EPS)[:, None] * query_gain
    key_n = key_f * lax.rsqrt(key_sq / D + EPS)[:, None] * key_gain
    cosine, sine_table = rope_tables(slot_count, HD)
    query_r = rotate(query_n.reshape(slot_count, head_count, HD), cosine, sine_table).astype(
        jnp.bfloat16
    )
    key_r = rotate(key_n.reshape(slot_count, head_count, HD), cosine, sine_table).astype(
        jnp.bfloat16
    )
    scores = jnp.einsum(
        "qhd,khd->hqk", query_r, key_r, preferred_element_type=jnp.float32
    ) * HD ** (-0.5)
    position = jnp.arange(slot_count, dtype=jnp.int32)
    allowed = (position[None, :] <= position[:, None]) & (position[None, :] < my_length)
    scores = jnp.where(allowed[None], scores, -jnp.inf)
    row_peak = jnp.max(scores, axis=2, keepdims=True)
    expd = jnp.exp(scores - row_peak)
    probabilities = (expd / jnp.sum(expd, axis=2, keepdims=True)).astype(jnp.bfloat16)
    value_heads = values.reshape(slot_count, head_count, HD)
    attended = jnp.einsum(
        "hqk,khd->qhd", probabilities, value_heads, preferred_element_type=jnp.float32
    )
    attended = attended.astype(jnp.bfloat16).reshape(slot_count, feature_count)
    attended_f = attended.astype(jnp.float32)
    attn_sq = lax.psum(jnp.sum(attended_f * attended_f, axis=1), "wt")
    layer_rows = (
        hidden_in.astype(jnp.float32)
        + attended_f * lax.rsqrt(attn_sq / D + EPS)[:, None] * attn_gain
    ).astype(jnp.bfloat16)
    live_mask = (position < my_length)[:, None]
    page_count = slot_count // PAGE
    zero_value = jnp.zeros((), jnp.bfloat16)
    key_pages = jnp.where(live_mask, key_r.reshape(slot_count, feature_count), zero_value).reshape(
        page_count, PAGE, feature_count
    )
    value_pages = jnp.where(live_mask, values, zero_value).reshape(page_count, PAGE, feature_count)
    placement = page_table[0]
    key_cache = jnp.zeros_like(key_pages).at[placement].set(key_pages)
    value_cache = jnp.zeros_like(value_pages).at[placement].set(value_pages)
    regrouped = deal_rows(layer_rows, owner_start, owner_len, device, owners, LIVE)
    regrouped, weights = lax.optimization_barrier((regrouped, weights))
    outer = lax.axis_size("ra")
    inner = lax.axis_size("rb")
    parts = lax.axis_size("wt")
    piece = lax.all_gather(regrouped.reshape(parts, LIVE // parts, feature_count), "ra", axis=1)
    stacked = jnp.einsum("wrtk,skn->wrtsn", piece, weights, preferred_element_type=jnp.float32)
    stacked = lax.all_to_all(stacked.astype(jnp.bfloat16), "wt", split_axis=0, concat_axis=0, tiled=True)
    summed = jnp.sum(stacked.astype(jnp.float32), axis=0)
    gated = (jax.nn.silu(summed[:, :, 0]) * summed[:, :, 1]).astype(jnp.bfloat16)
    rows_here = gated.shape[1]
    gated = gated.reshape(outer, rows_here, inner, unit_count)
    gated = lax.all_to_all(gated, "rb", split_axis=2, concat_axis=2, tiled=True)
    gated = jnp.transpose(gated, (0, 2, 1, 3)).reshape(outer * inner, rows_here, unit_count)
    return (gated, key_cache, value_cache)


def solution(mesh):
    inner = 16
    outer = mesh.shape["req"] // inner
    split = Mesh(mesh.devices.reshape(outer, inner, mesh.shape["wt"]), ("ra", "rb", "wt"))
    req = ("ra", "rb")
    placed = (
        P(req, "wt"),
        P(req, "wt"),
        P(req, "wt"),
        P(req, "wt"),
        P("wt"),
        P("wt"),
        P("wt"),
        P("wt", req),
        P("wt", req),
        P(),
        P(),
        P(req, None),
    )
    return jax.shard_map(
        per_device,
        mesh=split,
        in_specs=placed,
        out_specs=(P(None, "wt", req), P(req, None, "wt"), P(req, None, "wt")),
        check_vma=False,
    )
```
